256 devices in a mesh: dp: 8 (over y, core), mp: 32 (over z, x).
Axes of the slice: x: 4, y: 4, z: 8, core: 2. Of those that a mesh axis runs over, the one named last changes fastest.
Arguments:
- table: bfloat16 [32, 2048, 128], P('mp'), may hold values from -6 to 6
- ids: int32 [65536, 32, 2], P('dp', 'mp'), may hold values from 0 to 2047
- counts: int32 [256, 8], P(('dp', 'mp')), may hold values from 1 to 96, 256 in all within a row
- labels: int32 [65536], P(('dp', 'mp')), may hold values from 0 to 4
- request_home: int32 [2048], replicated, may hold values from 0 to 2047, each once
- user_codes: bfloat16 [2048, 1024], P('dp'), may hold values from -6 to 6
- cross_down: bfloat16 [4096, 256], replicated, may hold values from -0.09375 to 0.09375
- cross_up: bfloat16 [256, 4096], replicated, may hold values from -0.375 to 0.375
- cross_bias: float32 [4096], replicated, may hold values from -4 to 4
- tower_weight: bfloat16 [4096, 1024], P('mp'), may hold values from -0.09375 to 0.09375
- tower_bias: float32 [1024], replicated, may hold values from -3 to 3
Outputs:
- scores: float32 [65536], P(('dp', 'mp'))
- pooled_grad: bfloat16 [65536, 32, 128], P('dp', 'mp')
The draws below stay inside these ranges and needn't reach their ends.
Inputs may be any that keep to these rules, and one draw needn't show every extreme that they name: `counts`: each row sums to 256; its largest entry is exactly 96. `request_home`: a permutation of the request slots.
All inputs are finite; a program needn't handle non-finite values.
Results may differ from the reference program's by a relative error of at most 0.0097.
Values may be sent and summed in bfloat16 or wider, within the bound.
No kernel may reach another device: no remote copies, remote signals or barrier semaphores. Data moves between devices by JAX's collectives and lax.ppermute only.
A program may use at most 128 MiB of HBM per device.

```python
import math
import jax
import jax.numpy as jnp
import numpy as np
from jax import lax

EMB = 128
FEATURES = 32
D = 4096
R = 256
H = 1024
HOT = 2
TROWS = 2048
ROWS_DEV = 256
SEG_DEV = 8
MOST = 96
CAND = 65536
REQUESTS = 2048
N_DP = 8
N_MP = 32


def plant(entries, own_key, least, largest):
    index_at = [jax.random.randint(jax.random.fold_in(own_key, axis), (), 0, length) for axis, length in enumerate(entries.shape)]
    longest = entries.shape.index(max(entries.shape))
    neighbour = index_at[:longest] + [(index_at[longest] + 1) % entries.shape[longest]] + index_at[longest + 1:]
    return entries.at[tuple(index_at)].set(least).at[tuple(neighbour)].set(largest)


def block_levels(rng, shape, pieces, smallest, largest):
    factor_of, own = 1.0, jax.random.fold_in(rng, 6)
    for axis_at, shards_of in pieces:
        heights = jnp.exp(jax.random.uniform(jax.random.fold_in(own, axis_at), (shards_of,), jnp.float32, smallest / len(pieces), largest / len(pieces)))
        factor_of = factor_of * jnp.repeat(heights, shape[axis_at] // shards_of).reshape([-1 if axis == axis_at else 1 for axis in range(len(shape))])
    return factor_of


def split_up(number_of, total, bound, skew):
    loads = [(1 << 20) // math.isqrt(grade ** skew) + 1 for grade in range(2, number_of + 1)]
    rest, given = total - bound - (number_of - 1), [1] * (number_of - 1)
    while rest > 0:
        movable = [i for i in range(number_of - 1) if given[i] < bound]
        whole, budget = sum([loads[i] for i in movable]), rest
        for i in movable:
            addition = min(bound - given[i], max(1, budget * loads[i] // whole), rest)
            given[i] = given[i] + addition
            rest = rest - addition
    return np.array([bound] + given)


def uneven(rng, count, total, most, skew):
    if count == 2:
        one = jax.random.randint(rng, (), max(1, total - most), min(most, total - 1) + 1)
        return jnp.stack([one, total - one])
    tallies = jnp.asarray(split_up(count, total, most, skew), jnp.int32)
    twos = (count - 1) // 2
    source_of, taker = tallies[1:1 + 2 * twos:2], tallies[2:2 + 2 * twos:2]
    margin = jnp.minimum(source_of - 1, most - taker)
    moved = jax.random.randint(jax.random.fold_in(rng, 1), (twos,), 0, 1 << 20) % (margin + 1)
    tallies = tallies.at[1:1 + 2 * twos:2].set(source_of - moved).at[2:2 + 2 * twos:2].set(taker + moved)
    return tallies[jax.random.permutation(jax.random.fold_in(rng, 2), count)]


def centred(stream_key, extent, scale, bound, pieces=(), kind=jnp.bfloat16):
    values = jax.random.normal(stream_key, extent, jnp.float32) * scale
    if len(pieces) > 0:
        values = block_levels(stream_key, extent, pieces, -0.22, 0.18) * values
    return jnp.clip(values, min=-bound, max=bound).astype(kind)


def setup_inputs(seed: int = 0) -> dict:
    seeds = jax.random.split(jax.random.key(seed), 12)
    table = centred(seeds[0], (FEATURES, TROWS, EMB), 1.0, 6.0, ((0, 32),))
    ids = plant(jax.random.randint(seeds[1], (CAND, FEATURES, HOT), 0, TROWS), jax.random.fold_in(seeds[1], 1), 0, TROWS - 1).astype(jnp.int32)
    counts = jax.vmap(lambda own: uneven(own, SEG_DEV, ROWS_DEV, MOST, 2))(jax.random.split(seeds[2], (N_DP * N_MP))).reshape((N_DP * N_MP, SEG_DEV)).astype(jnp.int32)
    labels = plant(jax.random.randint(seeds[3], (CAND,), 0, 5), jax.random.fold_in(seeds[3], 1), 0, 4).astype(jnp.int32)
    request_home = jax.random.permutation(seeds[4], REQUESTS).astype(jnp.int32)
    user_codes = centred(seeds[5], (REQUESTS, H), 1.0, 6.0, ((0, 8),))
    cross_down = centred(seeds[6], (D, R), D ** -0.5, 0.09375)
    cross_up = centred(seeds[7], (R, D), R ** -0.5, 0.375)
    cross_bias = centred(seeds[8], (D,), 1.0, 4.0, (), jnp.float32)
    tower_weight = centred(seeds[9], (D, H), D ** -0.5, 0.09375, ((0, 32),))
    tower_bias = centred(seeds[10], (H,), 0.5, 3.0, (), jnp.float32)
    return dict(table=table, ids=ids, counts=counts, labels=labels, request_home=request_home, user_codes=user_codes, cross_down=cross_down, cross_up=cross_up, cross_bias=cross_bias, tower_weight=tower_weight, tower_bias=tower_bias)


def pool_rows(table, ids):
    feat = table.shape[0]
    picked = table[jnp.arange(feat, dtype=jnp.int32)[None, :, None], ids]
    return lax.optimization_barrier(jnp.sum(picked, axis=2, dtype=jnp.float32)).astype(table.dtype)

def members(counts_row, rows):
    ends = jnp.cumsum(counts_row).astype(jnp.int32)
    starts = ends - counts_row
    place = jnp.arange(rows, dtype=jnp.int32)[:, None]
    return (place >= starts[None, :]) & (place < ends[None, :])

def dot_last(left, right):
    return lax.dot_general(left, right, (((1,), (1,)), ((), ())), preferred_element_type=jnp.float32)

def pair_grad(scores, member, labels):
    gain = jnp.exp2(labels.astype(jnp.float32))
    member_f = member.astype(jnp.float32)
    same = jnp.dot(member_f, member_f.T) > 0.5
    diff = gain[:, None] - gain[None, :]
    gap = scores[None, :] - scores[:, None]
    turn = jnp.where(diff > 0, jax.nn.sigmoid(gap), jax.nn.sigmoid(-gap))
    total = lax.optimization_barrier(jnp.sum(jnp.where(same, diff * turn, 0.0), axis=1))
    seg_gain = lax.optimization_barrier(jnp.sum(jnp.where(member, (gain - 1.0)[:, None], 0.0), axis=0))
    norm = lax.optimization_barrier(jnp.sum(jnp.where(member, seg_gain[None, :], 0.0), axis=1))
    return -total / jnp.maximum(norm, 1.0)

def reference(table, ids, counts, labels, request_home, user_codes, cross_down, cross_up, cross_bias, tower_weight, tower_bias):
    blocks = counts.shape[0]
    seg_count = counts.shape[1]
    rows = labels.shape[0] // blocks
    total_req = request_home.shape[0]
    slot_req = jnp.zeros((total_req,), jnp.int32).at[request_home].set(jnp.arange(total_req, dtype=jnp.int32))
    slot_codes = user_codes[slot_req].reshape(blocks, seg_count, -1)
    ids_b = ids.reshape(blocks, rows, ids.shape[1], ids.shape[2])
    labels_b = labels.reshape(blocks, rows)
    width = user_codes.shape[1]
    scale = 1.0 / jnp.sqrt(jnp.float32(width))

    def one(items):
        ids_blk, counts_row, label_row, user_seg = items
        pooled = pool_rows(table, ids_blk)
        x0 = pooled.reshape(rows, -1)
        member = members(counts_row, rows)
        z = jnp.dot(x0, cross_down, preferred_element_type=jnp.float32).astype(jnp.bfloat16)
        cross = jnp.dot(z, cross_up, preferred_element_type=jnp.float32) + cross_bias
        x1 = (x0 * cross + x0).astype(jnp.bfloat16)
        act = jnp.dot(x1, tower_weight, preferred_element_type=jnp.float32) + tower_bias
        sig = jax.nn.sigmoid(act)
        hidden = (act * sig).astype(jnp.bfloat16)
        pair = dot_last(hidden, user_seg)
        score = lax.optimization_barrier(jnp.sum(jnp.where(member, pair, 0.0), axis=1)) * scale
        dscore = pair_grad(score, member, label_row)
        code = jnp.dot(member.astype(jnp.bfloat16), user_seg, preferred_element_type=jnp.float32)
        slope = sig * (1.0 + act * (1.0 - sig))
        dact = (dscore[:, None] * code * scale * slope).astype(jnp.bfloat16)
        dx1 = dot_last(dact, tower_weight)
        dcross = (dx1 * x0).astype(jnp.bfloat16)
        dz = dot_last(dcross, cross_up).astype(jnp.bfloat16)
        dx0 = dx1 * (1.0 + cross) + dot_last(dz, cross_down)
        return (score, dx0.astype(jnp.bfloat16).reshape(pooled.shape))
    scores, grads = lax.map(one, (ids_b, counts, labels_b, slot_codes))
    return (scores.reshape(-1), grads.reshape(ids.shape[0], ids.shape[1], -1))
```

```python
import jax
import jax.numpy as jnp
from jax import lax
from jax.sharding import PartitionSpec as P


def members(counts_row, rows):
    ends = jnp.cumsum(counts_row)
    starts = ends - counts_row
    place = jnp.arange(rows, dtype=jnp.int32)[:, None]
    return (place >= starts[None, :]) & (place < ends[None, :])


def dot_last(left, right):
    return lax.dot_general(
        left, right, (((1,), (1,)), ((), ())), preferred_element_type=jnp.float32
    )


def pair_grad(scores, member, labels):
    gain = jnp.exp2(labels.astype(jnp.float32))
    member_f = member.astype(jnp.float32)
    same = jnp.dot(member_f, member_f.T) > 0.5
    diff = gain[:, None] - gain[None, :]
    gap = scores[None, :] - scores[:, None]
    turn = jnp.where(diff > 0, jax.nn.sigmoid(gap), jax.nn.sigmoid(-gap))
    total = jnp.sum(jnp.where(same, diff * turn, 0.0), axis=1)
    seg_gain = jnp.sum(jnp.where(member, (gain - 1.0)[:, None], 0.0), axis=0)
    norm = jnp.sum(jnp.where(member, seg_gain[None, :], 0.0), axis=1)
    return -total / jnp.maximum(norm, 1.0)


def local(
    table,
    ids,
    counts,
    labels,
    request_home,
    user_codes,
    cross_down,
    cross_up,
    cross_bias,
    tower_weight,
    tower_bias,
):
    f32, bf16 = jnp.float32, jnp.bfloat16
    n_mp = lax.axis_size("mp")
    n_dp = lax.axis_size("dp")
    d_idx = lax.axis_index("dp")
    m_idx = lax.axis_index("mp")
    rows = labels.shape[0]
    seg_count = counts.shape[1]
    width = user_codes.shape[1]
    emb = table.shape[2]
    rank = cross_down.shape[1]
    scale = 1.0 / jnp.sqrt(jnp.float32(width))

    piece = tower_weight.shape[1] // n_dp
    w_piece = lax.dynamic_slice_in_dim(tower_weight, d_idx * piece, piece, axis=1)
    w_cols = lax.all_gather(w_piece, "mp", axis=0, tiled=True)
    w_all = lax.all_gather(w_cols, "dp", axis=1, tiled=True)
    w3 = w_all.reshape(n_mp, emb, width)

    held = user_codes.shape[0]
    home_local = lax.dynamic_slice_in_dim(request_home, d_idx * held, held)
    wanted = (
        (jnp.arange(n_dp, dtype=jnp.int32)[:, None] * n_mp + m_idx) * seg_count
        + jnp.arange(seg_count, dtype=jnp.int32)[None, :]
    ).reshape(-1)
    pick = (home_local[None, :] == wanted[:, None]).astype(bf16)
    mine = jnp.dot(pick, user_codes, preferred_element_type=f32).astype(bf16)
    user_seg = lax.psum_scatter(
        mine.reshape(n_dp, seg_count, width), "dp", scatter_dimension=0, tiled=False
    )

    slab = table[0]
    picked = jnp.take(slab, ids[:, 0, :], axis=0, mode="clip")
    pooled = jnp.sum(picked.astype(f32), axis=1).astype(bf16)
    x0f = lax.all_to_all(
        pooled.reshape(n_mp, rows, emb), "mp", split_axis=0, concat_axis=0, tiled=True
    )

    member = members(counts[0], rows)
    cd3 = cross_down.reshape(n_mp, emb, rank)
    cu3 = cross_up.reshape(rank, n_mp, emb)
    bias3 = cross_bias.reshape(n_mp, 1, emb)
    z = jnp.einsum("fcd,fdr->cr", x0f, cd3, preferred_element_type=f32).astype(bf16)
    cross = jnp.einsum("cr,rfd->fcd", z, cu3, preferred_element_type=f32) + bias3
    x1 = (x0f * cross + x0f).astype(bf16)
    act = jnp.einsum("fcd,fdh->ch", x1, w3, preferred_element_type=f32) + tower_bias
    sig = jax.nn.sigmoid(act)
    hidden = (act * sig).astype(bf16)
    pair = dot_last(hidden, user_seg)
    score = jnp.sum(jnp.where(member, pair, 0.0), axis=1) * scale
    dscore = pair_grad(score, member, labels)
    code = jnp.dot(member.astype(bf16), user_seg, preferred_element_type=f32)
    slope = sig * (1.0 + act * (1.0 - sig))
    dact = (dscore[:, None] * code * scale * slope).astype(bf16)
    dx1 = jnp.einsum("ch,fdh->fcd", dact, w3, preferred_element_type=f32)
    dcross = (dx1 * x0f).astype(bf16)
    dz = jnp.einsum("fcd,rfd->cr", dcross, cu3, preferred_element_type=f32).astype(bf16)
    dx0 = dx1 * (1.0 + cross) + jnp.einsum(
        "cr,fdr->fcd", dz, cd3, preferred_element_type=f32
    )
    grads = dx0.astype(bf16)
    returned = lax.all_to_all(grads, "mp", split_axis=0, concat_axis=0, tiled=True)
    return (score, returned.reshape(n_mp * rows, 1, emb))


def solution(mesh):
    in_specs = (
        P("mp", None, None),
        P("dp", "mp", None),
        P(("dp", "mp"), None),
        P(("dp", "mp")),
        P(),
        P("dp", None),
        P(),
        P(),
        P(),
        P("mp", None),
        P(),
    )
    out_specs = (P(("dp", "mp")), P("dp", "mp", None))
    return jax.shard_map(local, mesh=mesh, in_specs=in_specs, out_specs=out_specs, check_vma=False)
```

```python
import jax
import jax.numpy as jnp
from jax import lax
from jax.experimental import pallas as pl
from jax.experimental.pallas import tpu as pltpu
from jax.sharding import PartitionSpec as P


def pool_kernel(ids_ref, tab_ref, out_ref, tabf, acc):
    step = pl.program_id(0)
    blk = out_ref.shape[0]
    total = ids_ref.shape[0] // 2

    @pl.when(step == 0)
    def _():
        tabf[...] = tab_ref[...].astype(jnp.float32)

    base = step * blk

    def body(j, carry):
        for u in range(8):
            c = j * 8 + u
            a = ids_ref[base + c]
            b = ids_ref[total + base + c]
            acc[pl.ds(c, 1), :] = tabf[pl.ds(a, 1), :] + tabf[pl.ds(b, 1), :]
        return carry

    lax.fori_loop(0, blk // 8, body, 0)
    out_ref[...] = acc[...].astype(out_ref.dtype)


def pool_rows(slab, flat_ids, count, blk=1024):
    slab_rows, emb = slab.shape
    spec = pltpu.PrefetchScalarGridSpec(
        num_scalar_prefetch=1,
        grid=(count // blk,),
        in_specs=[pl.BlockSpec((slab_rows, emb), lambda i, ids: (0, 0))],
        out_specs=pl.BlockSpec((blk, emb), lambda i, ids: (i, 0)),
        scratch_shapes=[
            pltpu.VMEM((slab_rows, emb), jnp.float32),
            pltpu.VMEM((blk, emb), jnp.float32),
        ],
    )
    return pl.pallas_call(
        pool_kernel,
        grid_spec=spec,
        out_shape=jax.ShapeDtypeStruct((count, emb), slab.dtype),
    )(flat_ids, slab)


def members(counts_row, rows):
    ends = jnp.cumsum(counts_row)
    starts = ends - counts_row
    place = jnp.arange(rows, dtype=jnp.int32)[:, None]
    return (place >= starts[None, :]) & (place < ends[None, :])


def dot_last(left, right):
    return lax.dot_general(
        left, right, (((1,), (1,)), ((), ())), preferred_element_type=jnp.float32
    )


def pair_grad(scores, member, labels):
    gain = jnp.exp2(labels.astype(jnp.float32))
    member_f = member.astype(jnp.float32)
    same = jnp.dot(member_f, member_f.T) > 0.5
    diff = gain[:, None] - gain[None, :]
    gap = scores[None, :] - scores[:, None]
    turn = jnp.where(diff > 0, jax.nn.sigmoid(gap), jax.nn.sigmoid(-gap))
    total = jnp.sum(jnp.where(same, diff * turn, 0.0), axis=1)
    seg_gain = jnp.sum(jnp.where(member, (gain - 1.0)[:, None], 0.0), axis=0)
    norm = jnp.sum(jnp.where(member, seg_gain[None, :], 0.0), axis=1)
    return -total / jnp.maximum(norm, 1.0)


def local(
    table,
    ids,
    counts,
    labels,
    request_home,
    user_codes,
    cross_down,
    cross_up,
    cross_bias,
    tower_weight,
    tower_bias,
):
    f32, bf16 = jnp.float32, jnp.bfloat16
    n_mp = lax.axis_size("mp")
    n_dp = lax.axis_size("dp")
    d_idx = lax.axis_index("dp")
    m_idx = lax.axis_index("mp")
    rows = labels.shape[0]
    seg_count = counts.shape[1]
    width = user_codes.shape[1]
    emb = table.shape[2]
    rank = cross_down.shape[1]
    scale = 1.0 / jnp.sqrt(jnp.float32(width))

    piece = tower_weight.shape[1] // n_dp
    w_piece = lax.dynamic_slice_in_dim(tower_weight, d_idx * piece, piece, axis=1)
    w_cols = lax.all_to_all(
        jnp.broadcast_to(w_piece[None], (n_mp,) + w_piece.shape),
        "mp", split_axis=0, concat_axis=0, tiled=True,
    ).reshape(n_mp * w_piece.shape[0], piece)
    w_all = lax.all_gather(w_cols, "dp", axis=1, tiled=True)
    w3 = w_all.reshape(n_mp, emb, width)

    held = user_codes.shape[0]
    home_local = lax.dynamic_slice_in_dim(request_home, d_idx * held, held)
    wanted = (
        (jnp.arange(n_dp, dtype=jnp.int32)[:, None] * n_mp + m_idx) * seg_count
        + jnp.arange(seg_count, dtype=jnp.int32)[None, :]
    ).reshape(-1)
    pick = (home_local[None, :] == wanted[:, None]).astype(bf16)
    mine = jnp.dot(pick, user_codes, preferred_element_type=f32).astype(bf16)
    user_seg = lax.psum_scatter(
        mine.reshape(n_dp, seg_count, width), "dp", scatter_dimension=0, tiled=False
    )

    count = ids.shape[0]
    flat_ids = jnp.transpose(ids[:, 0, :]).reshape(-1)
    pooled = pool_rows(table[0], flat_ids, count)
    x0f = lax.all_to_all(
        pooled.reshape(n_mp, rows, emb), "mp", split_axis=0, concat_axis=0, tiled=True
    )

    member = members(counts[0], rows)
    cd3 = cross_down.reshape(n_mp, emb, rank)
    cu3 = cross_up.reshape(rank, n_mp, emb)
    bias3 = cross_bias.reshape(n_mp, 1, emb)
    z = jnp.einsum("fcd,fdr->cr", x0f, cd3, preferred_element_type=f32).astype(bf16)
    cross = jnp.einsum("cr,rfd->fcd", z, cu3, preferred_element_type=f32) + bias3
    x1 = (x0f * cross + x0f).astype(bf16)
    act = jnp.einsum("fcd,fdh->ch", x1, w3, preferred_element_type=f32) + tower_bias
    sig = jax.nn.sigmoid(act)
    hidden = (act * sig).astype(bf16)
    pair = dot_last(hidden, user_seg)
    score = jnp.sum(jnp.where(member, pair, 0.0), axis=1) * scale
    dscore = pair_grad(score, member, labels)
    code = jnp.dot(member.astype(bf16), user_seg, preferred_element_type=f32)
    slope = sig * (1.0 + act * (1.0 - sig))
    dact = (dscore[:, None] * code * scale * slope).astype(bf16)
    dx1 = jnp.einsum("ch,fdh->fcd", dact, w3, preferred_element_type=f32)
    dcross = (dx1 * x0f).astype(bf16)
    dz = jnp.einsum("fcd,rfd->cr", dcross, cu3, preferred_element_type=f32).astype(bf16)
    dx0 = dx1 * (1.0 + cross) + jnp.einsum(
        "cr,fdr->fcd", dz, cd3, preferred_element_type=f32
    )
    grads = dx0.astype(bf16)
    returned = lax.all_to_all(grads, "mp", split_axis=0, concat_axis=0, tiled=True)
    return (score, returned.reshape(n_mp * rows, 1, emb))


def solution(mesh):
    in_specs = (
        P("mp", None, None),
        P("dp", "mp", None),
        P(("dp", "mp"), None),
        P(("dp", "mp")),
        P(),
        P("dp", None),
        P(),
        P(),
        P(),
        P("mp", None),
        P(),
    )
    out_specs = (P(("dp", "mp")), P("dp", "mp", None))
    return jax.shard_map(local, mesh=mesh, in_specs=in_specs, out_specs=out_specs, check_vma=False)
```

```python
import jax
import jax.numpy as jnp
from jax import lax
from jax.experimental import pallas as pl
from jax.experimental.pallas import tpu as pltpu
from jax.sharding import PartitionSpec as P


def pool_kernel(ids_ref, tab_ref, out_ref, tabf, acc):
    step = pl.program_id(0)
    blk = out_ref.shape[0]
    total = ids_ref.shape[0] // 2

    @pl.when(step == 0)
    def _():
        tabf[...] = tab_ref[...].astype(jnp.float32)

    base = step * blk

    def body(j, carry):
        for u in range(8):
            c = j * 8 + u
            a = ids_ref[base + c]
            b = ids_ref[total + base + c]
            acc[pl.ds(c, 1), :] = tabf[pl.ds(a, 1), :] + tabf[pl.ds(b, 1), :]
        return carry

    lax.fori_loop(0, blk // 8, body, 0)
    out_ref[...] = acc[...].astype(out_ref.dtype)


def pool_rows(slab, flat_ids, count, blk=1024):
    slab_rows, emb = slab.shape
    spec = pltpu.PrefetchScalarGridSpec(
        num_scalar_prefetch=1,
        grid=(count // blk,),
        in_specs=[pl.BlockSpec((slab_rows, emb), lambda i, ids: (0, 0))],
        out_specs=pl.BlockSpec((blk, emb), lambda i, ids: (i, 0)),
        scratch_shapes=[
            pltpu.VMEM((slab_rows, emb), jnp.float32),
            pltpu.VMEM((blk, emb), jnp.float32),
        ],
    )
    return pl.pallas_call(
        pool_kernel,
        grid_spec=spec,
        out_shape=jax.ShapeDtypeStruct((count, emb), slab.dtype),
    )(flat_ids, slab)


def members(counts_row, rows):
    ends = jnp.cumsum(counts_row)
    starts = ends - counts_row
    place = jnp.arange(rows, dtype=jnp.int32)[:, None]
    return (place >= starts[None, :]) & (place < ends[None, :])


def dot_last(left, right):
    return lax.dot_general(
        left, right, (((1,), (1,)), ((), ())), preferred_element_type=jnp.float32
    )


def pair_grad(scores, member, labels):
    gain = jnp.exp2(labels.astype(jnp.float32))
    member_f = member.astype(jnp.float32)
    same = jnp.dot(member_f, member_f.T) > 0.5
    diff = gain[:, None] - gain[None, :]
    gap = scores[None, :] - scores[:, None]
    turn = jnp.where(diff > 0, jax.nn.sigmoid(gap), jax.nn.sigmoid(-gap))
    total = jnp.sum(jnp.where(same, diff * turn, 0.0), axis=1)
    seg_gain = jnp.sum(jnp.where(member, (gain - 1.0)[:, None], 0.0), axis=0)
    norm = jnp.sum(jnp.where(member, seg_gain[None, :], 0.0), axis=1)
    return -total / jnp.maximum(norm, 1.0)


def local(
    table,
    ids,
    counts,
    labels,
    request_home,
    user_codes,
    cross_down,
    cross_up,
    cross_bias,
    tower_weight,
    tower_bias,
):
    f32, bf16 = jnp.float32, jnp.bfloat16
    n_mp = lax.axis_size("mp")
    n_dp = lax.axis_size("dp")
    d_idx = lax.axis_index("dp")
    m_idx = lax.axis_index("mp")
    rows = labels.shape[0]
    seg_count = counts.shape[1]
    width = user_codes.shape[1]
    emb = table.shape[2]
    rank = cross_down.shape[1]
    scale = 1.0 / jnp.sqrt(jnp.float32(width))

    piece = tower_weight.shape[1] // n_dp
    w_piece = lax.dynamic_slice_in_dim(tower_weight, d_idx * piece, piece, axis=1)
    got = [w_piece]
    for shift in range(1, n_mp):
        pairs = [(j, (j + shift) % n_mp) for j in range(n_mp)]
        got.append(lax.ppermute(w_piece, "mp", pairs))

    held = user_codes.shape[0]
    home_local = lax.dynamic_slice_in_dim(request_home, d_idx * held, held)
    wanted = (
        (jnp.arange(n_dp, dtype=jnp.int32)[:, None] * n_mp + m_idx) * seg_count
        + jnp.arange(seg_count, dtype=jnp.int32)[None, :]
    ).reshape(-1)
    pick = (home_local[None, :] == wanted[:, None]).astype(bf16)
    mine = jnp.dot(pick, user_codes, preferred_element_type=f32).astype(bf16)
    user_seg = lax.psum_scatter(
        mine.reshape(n_dp, seg_count, width), "dp", scatter_dimension=0, tiled=False
    )

    count = ids.shape[0]
    flat_ids = jnp.transpose(ids[:, 0, :]).reshape(-1)
    pooled = pool_rows(table[0], flat_ids, count)
    w_stack, pooled = lax.optimization_barrier((jnp.stack(got), pooled))
    order = (m_idx - jnp.arange(n_mp, dtype=jnp.int32)) % n_mp
    w_cols = jnp.take(w_stack, order, axis=0, mode="clip")
    w_cols = w_cols.reshape(n_mp * w_piece.shape[0], piece)
    w_all = lax.all_gather(w_cols, "dp", axis=1, tiled=True)
    w3 = w_all.reshape(n_mp, emb, width)
    x0f = lax.all_to_all(
        pooled.reshape(n_mp, rows, emb), "mp", split_axis=0, concat_axis=0, tiled=True
    )

    member = members(counts[0], rows)
    cd3 = cross_down.reshape(n_mp, emb, rank)
    cu3 = cross_up.reshape(rank, n_mp, emb)
    bias3 = cross_bias.reshape(n_mp, 1, emb)
    z = jnp.einsum("fcd,fdr->cr", x0f, cd3, preferred_element_type=f32).astype(bf16)
    cross = jnp.einsum("cr,rfd->fcd", z, cu3, preferred_element_type=f32) + bias3
    x1 = (x0f * cross + x0f).astype(bf16)
    act = jnp.einsum("fcd,fdh->ch", x1, w3, preferred_element_type=f32) + tower_bias
    sig = jax.nn.sigmoid(act)
    hidden = (act * sig).astype(bf16)
    pair = dot_last(hidden, user_seg)
    score = jnp.sum(jnp.where(member, pair, 0.0), axis=1) * scale
    dscore = pair_grad(score, member, labels)
    code = jnp.dot(member.astype(bf16), user_seg, preferred_element_type=f32)
    slope = sig * (1.0 + act * (1.0 - sig))
    dact = (dscore[:, None] * code * scale * slope).astype(bf16)
    dx1 = jnp.einsum("ch,fdh->fcd", dact, w3, preferred_element_type=f32)
    dcross = (dx1 * x0f).astype(bf16)
    dz = jnp.einsum("fcd,rfd->cr", dcross, cu3, preferred_element_type=f32).astype(bf16)
    dx0 = dx1 * (1.0 + cross) + jnp.einsum(
        "cr,fdr->fcd", dz, cd3, preferred_element_type=f32
    )
    grads = dx0.astype(bf16)
    returned = lax.all_to_all(grads, "mp", split_axis=0, concat_axis=0, tiled=True)
    return (score, returned.reshape(n_mp * rows, 1, emb))


def solution(mesh):
    in_specs = (
        P("mp", None, None),
        P("dp", "mp", None),
        P(("dp", "mp"), None),
        P(("dp", "mp")),
        P(),
        P("dp", None),
        P(),
        P(),
        P(),
        P("mp", None),
        P(),
    )
    out_specs = (P(("dp", "mp")), P("dp", "mp", None))
    return jax.shard_map(local, mesh=mesh, in_specs=in_specs, out_specs=out_specs, check_vma=False)
```

```python
import jax
import jax.numpy as jnp
from jax import lax
from jax.experimental import pallas as pl
from jax.experimental.pallas import tpu as pltpu
from jax.sharding import Mesh, PartitionSpec as P


def pool_kernel(ids_ref, tab_ref, out_ref, tabf, acc):
    step = pl.program_id(0)
    blk = out_ref.shape[0]
    total = ids_ref.shape[0] // 2

    @pl.when(step == 0)
    def _():
        tabf[...] = tab_ref[...].astype(jnp.float32)

    base = step * blk

    def body(j, carry):
        for u in range(8):
            c = j * 8 + u
            a = ids_ref[base + c]
            b = ids_ref[total + base + c]
            acc[pl.ds(c, 1), :] = tabf[pl.ds(a, 1), :] + tabf[pl.ds(b, 1), :]
        return carry

    lax.fori_loop(0, blk // 8, body, 0)
    out_ref[...] = acc[...].astype(out_ref.dtype)


def pool_rows(slab, flat_ids, count, blk=1024):
    slab_rows, emb = slab.shape
    spec = pltpu.PrefetchScalarGridSpec(
        num_scalar_prefetch=1,
        grid=(count // blk,),
        in_specs=[pl.BlockSpec((slab_rows, emb), lambda i, ids: (0, 0))],
        out_specs=pl.BlockSpec((blk, emb), lambda i, ids: (i, 0)),
        scratch_shapes=[
            pltpu.VMEM((slab_rows, emb), jnp.float32),
            pltpu.VMEM((blk, emb), jnp.float32),
        ],
    )
    return pl.pallas_call(
        pool_kernel,
        grid_spec=spec,
        out_shape=jax.ShapeDtypeStruct((count, emb), slab.dtype),
    )(flat_ids, slab)


def members(counts_row, rows):
    ends = jnp.cumsum(counts_row)
    starts = ends - counts_row
    place = jnp.arange(rows, dtype=jnp.int32)[:, None]
    return (place >= starts[None, :]) & (place < ends[None, :])


def dot_last(left, right):
    return lax.dot_general(
        left, right, (((1,), (1,)), ((), ())), preferred_element_type=jnp.float32
    )


def pair_grad(scores, member, labels):
    gain = jnp.exp2(labels.astype(jnp.float32))
    member_f = member.astype(jnp.float32)
    same = jnp.dot(member_f, member_f.T) > 0.5
    diff = gain[:, None] - gain[None, :]
    gap = scores[None, :] - scores[:, None]
    turn = jnp.where(diff > 0, jax.nn.sigmoid(gap), jax.nn.sigmoid(-gap))
    total = jnp.sum(jnp.where(same, diff * turn, 0.0), axis=1)
    seg_gain = jnp.sum(jnp.where(member, (gain - 1.0)[:, None], 0.0), axis=0)
    norm = jnp.sum(jnp.where(member, seg_gain[None, :], 0.0), axis=1)
    return -total / jnp.maximum(norm, 1.0)


DP = ("y", "c")
MP = ("z", "x")


def a2a_mp(v, nz, nx):
    shape = v.shape
    v = v.reshape((nz, nx) + shape[1:])
    v = lax.all_to_all(v, "x", split_axis=1, concat_axis=1, tiled=True)
    v = lax.all_to_all(v, "z", split_axis=0, concat_axis=0, tiled=True)
    return v.reshape(shape)


def gather_mp(v, nz, nx):
    v = jnp.broadcast_to(v[None], (nx,) + v.shape)
    v = lax.all_to_all(v, "x", split_axis=0, concat_axis=0, tiled=True)
    v = jnp.broadcast_to(v[None], (nz,) + v.shape)
    v = lax.all_to_all(v, "z", split_axis=0, concat_axis=0, tiled=True)
    return v.reshape((nz * nx,) + v.shape[2:])


def local(
    table,
    ids,
    counts,
    labels,
    request_home,
    user_codes,
    cross_down,
    cross_up,
    cross_bias,
    tower_weight,
    tower_bias,
):
    f32, bf16 = jnp.float32, jnp.bfloat16
    nz, nx = lax.axis_size("z"), lax.axis_size("x")
    n_mp = nz * nx
    n_dp = lax.axis_size("y") * lax.axis_size("c")
    d_idx = lax.axis_index("y") * lax.axis_size("c") + lax.axis_index("c")
    m_idx = lax.axis_index("z") * nx + lax.axis_index("x")
    rows = labels.shape[0]
    seg_count = counts.shape[1]
    width = user_codes.shape[1]
    emb = table.shape[2]
    rank = cross_down.shape[1]
    scale = 1.0 / jnp.sqrt(jnp.float32(width))

    piece = tower_weight.shape[1] // n_dp
    w_piece = lax.dynamic_slice_in_dim(tower_weight, d_idx * piece, piece, axis=1)
    w_cols = gather_mp(w_piece, nz, nx).reshape(n_mp * w_piece.shape[0], piece)
    w_all = lax.all_gather(w_cols, DP, axis=1, tiled=True)
    w3 = w_all.reshape(n_mp, emb, width)

    held = user_codes.shape[0]
    home_local = lax.dynamic_slice_in_dim(request_home, d_idx * held, held)
    wanted = (
        (jnp.arange(n_dp, dtype=jnp.int32)[:, None] * n_mp + m_idx) * seg_count
        + jnp.arange(seg_count, dtype=jnp.int32)[None, :]
    ).reshape(-1)
    pick = (home_local[None, :] == wanted[:, None]).astype(bf16)
    mine = jnp.dot(pick, user_codes, preferred_element_type=f32).astype(bf16)
    user_seg = lax.psum_scatter(
        mine.reshape(n_dp, seg_count, width), DP, scatter_dimension=0, tiled=False
    )

    count = ids.shape[0]
    flat_ids = jnp.transpose(ids[:, 0, :]).reshape(-1)
    pooled = pool_rows(table[0], flat_ids, count)
    x0f = a2a_mp(pooled.reshape(n_mp, rows, emb), nz, nx)

    member = members(counts[0], rows)
    cd3 = cross_down.reshape(n_mp, emb, rank)
    cu3 = cross_up.reshape(rank, n_mp, emb)
    bias3 = cross_bias.reshape(n_mp, 1, emb)
    z = jnp.einsum("fcd,fdr->cr", x0f, cd3, preferred_element_type=f32).astype(bf16)
    cross = jnp.einsum("cr,rfd->fcd", z, cu3, preferred_element_type=f32) + bias3
    x1 = (x0f * cross + x0f).astype(bf16)
    act = jnp.einsum("fcd,fdh->ch", x1, w3, preferred_element_type=f32) + tower_bias
    sig = jax.nn.sigmoid(act)
    hidden = (act * sig).astype(bf16)
    pair = dot_last(hidden, user_seg)
    score = jnp.sum(jnp.where(member, pair, 0.0), axis=1) * scale
    dscore = pair_grad(score, member, labels)
    code = jnp.dot(member.astype(bf16), user_seg, preferred_element_type=f32)
    slope = sig * (1.0 + act * (1.0 - sig))
    dact = (dscore[:, None] * code * scale * slope).astype(bf16)
    dx1 = jnp.einsum("ch,fdh->fcd", dact, w3, preferred_element_type=f32)
    dcross = (dx1 * x0f).astype(bf16)
    dz = jnp.einsum("fcd,rfd->cr", dcross, cu3, preferred_element_type=f32).astype(bf16)
    dx0 = dx1 * (1.0 + cross) + jnp.einsum(
        "cr,fdr->fcd", dz, cd3, preferred_element_type=f32
    )
    grads = dx0.astype(bf16)
    returned = a2a_mp(grads, nz, nx)
    return (score, returned.reshape(n_mp * rows, 1, emb))


def split_mesh(mesh):
    grid = mesh.devices
    n_dp, n_mp = grid.shape
    try:
        nx = len({d.coords[0] for d in grid[0, :]})
        nc = len({d.core_on_chip for d in grid[:, 0]})
    except AttributeError:
        nx, nc = 1, 1
    if n_mp % nx or n_dp % nc:
        nx, nc = 1, 1
    return Mesh(grid.reshape(n_dp // nc, nc, n_mp // nx, nx), ("y", "c", "z", "x"))


def solution(mesh):
    mesh4 = split_mesh(mesh)
    in_specs = (
        P(MP, None, None),
        P(DP, MP, None),
        P(DP + MP, None),
        P(DP + MP),
        P(),
        P(DP, None),
        P(),
        P(),
        P(),
        P(MP, None),
        P(),
    )
    out_specs = (P(DP + MP), P(DP, MP, None))
    return jax.shard_map(local, mesh=mesh4, in_specs=in_specs, out_specs=out_specs, check_vma=False)
```

```python
import jax
import jax.numpy as jnp
from jax import lax
from jax.experimental import pallas as pl
from jax.experimental.pallas import tpu as pltpu
from jax.sharding import Mesh, PartitionSpec as P


def pool_kernel(ids_ref, tab_ref, out_ref, tabf, acc):
    step = pl.program_id(0)
    blk = out_ref.shape[0]
    total = ids_ref.shape[0] // 2

    @pl.when(step == 0)
    def _():
        tabf[...] = tab_ref[...].astype(jnp.float32)

    base = step * blk

    def body(j, carry):
        for u in range(8):
            c = j * 8 + u
            a = ids_ref[base + c]
            b = ids_ref[total + base + c]
            acc[pl.ds(c, 1), :] = tabf[pl.ds(a, 1), :] + tabf[pl.ds(b, 1), :]
        return carry

    lax.fori_loop(0, blk // 8, body, 0)
    out_ref[...] = acc[...].astype(out_ref.dtype)


def pool_rows(slab, flat_ids, count, blk=1024):
    slab_rows, emb = slab.shape
    spec = pltpu.PrefetchScalarGridSpec(
        num_scalar_prefetch=1,
        grid=(count // blk,),
        in_specs=[pl.BlockSpec((slab_rows, emb), lambda i, ids: (0, 0))],
        out_specs=pl.BlockSpec((blk, emb), lambda i, ids: (i, 0)),
        scratch_shapes=[
            pltpu.VMEM((slab_rows, emb), jnp.float32),
            pltpu.VMEM((blk, emb), jnp.float32),
        ],
    )
    return pl.pallas_call(
        pool_kernel,
        grid_spec=spec,
        out_shape=jax.ShapeDtypeStruct((count, emb), slab.dtype),
    )(flat_ids, slab)


def members(counts_row, rows):
    ends = jnp.cumsum(counts_row)
    starts = ends - counts_row
    place = jnp.arange(rows, dtype=jnp.int32)[:, None]
    return (place >= starts[None, :]) & (place < ends[None, :])


def dot_last(left, right):
    return lax.dot_general(
        left, right, (((1,), (1,)), ((), ())), preferred_element_type=jnp.float32
    )


def pair_grad(scores, member, labels):
    gain = jnp.exp2(labels.astype(jnp.float32))
    member_f = member.astype(jnp.float32)
    same = jnp.dot(member_f, member_f.T) > 0.5
    diff = gain[:, None] - gain[None, :]
    gap = scores[None, :] - scores[:, None]
    turn = jnp.where(diff > 0, jax.nn.sigmoid(gap), jax.nn.sigmoid(-gap))
    total = jnp.sum(jnp.where(same, diff * turn, 0.0), axis=1)
    seg_gain = jnp.sum(jnp.where(member, (gain - 1.0)[:, None], 0.0), axis=0)
    norm = jnp.sum(jnp.where(member, seg_gain[None, :], 0.0), axis=1)
    return -total / jnp.maximum(norm, 1.0)


DP = ("y", "c")
MP = ("z", "x")


def a2a_mp(v, nz, nx):
    shape = v.shape
    v = v.reshape((nz, nx) + shape[1:])
    v = lax.all_to_all(v, "x", split_axis=1, concat_axis=1, tiled=True)
    v = lax.all_to_all(v, "z", split_axis=0, concat_axis=0, tiled=True)
    return v.reshape(shape)


def gather_mp(v, nz, nx):
    v = jnp.broadcast_to(v[None], (nx,) + v.shape)
    v = lax.all_to_all(v, "x", split_axis=0, concat_axis=0, tiled=True)
    v = jnp.broadcast_to(v[None], (nz,) + v.shape)
    v = lax.all_to_all(v, "z", split_axis=0, concat_axis=0, tiled=True)
    return v.reshape((nz * nx,) + v.shape[2:])


def local(
    table,
    ids,
    counts,
    labels,
    request_home,
    user_codes,
    cross_down,
    cross_up,
    cross_bias,
    tower_weight,
    tower_bias,
):
    f32, bf16 = jnp.float32, jnp.bfloat16
    nz, nx = lax.axis_size("z"), lax.axis_size("x")
    n_mp = nz * nx
    n_dp = lax.axis_size("y") * lax.axis_size("c")
    d_idx = lax.axis_index("y") * lax.axis_size("c") + lax.axis_index("c")
    m_idx = lax.axis_index("z") * nx + lax.axis_index("x")
    rows = labels.shape[0]
    seg_count = counts.shape[1]
    width = user_codes.shape[1]
    emb = table.shape[2]
    rank = cross_down.shape[1]
    scale = 1.0 / jnp.sqrt(jnp.float32(width))

    piece = tower_weight.shape[1] // n_dp
    w_piece = lax.dynamic_slice_in_dim(tower_weight, d_idx * piece, piece, axis=1)
    w_x = lax.all_gather(w_piece, "x", axis=0, tiled=True)
    w_cols = lax.all_gather(w_x, "z", axis=0, tiled=True)

    held = user_codes.shape[0]
    home_local = lax.dynamic_slice_in_dim(request_home, d_idx * held, held)
    wanted = (
        (jnp.arange(n_dp, dtype=jnp.int32)[:, None] * n_mp + m_idx) * seg_count
        + jnp.arange(seg_count, dtype=jnp.int32)[None, :]
    ).reshape(-1)
    pick = (home_local[None, :] == wanted[:, None]).astype(bf16)
    mine = jnp.dot(pick, user_codes, preferred_element_type=f32).astype(bf16)
    sent = lax.all_to_all(mine.reshape(n_dp, seg_count, width), DP, 0, 0, tiled=True)
    user_seg = jnp.sum(sent.astype(f32), axis=0).astype(bf16)

    count = ids.shape[0]
    flat_ids = jnp.transpose(ids[:, 0, :]).reshape(-1)
    pooled = pool_rows(table[0], flat_ids, count)
    w_cols, pooled = lax.optimization_barrier((w_cols, pooled))
    w_all = lax.all_gather(w_cols, DP, axis=1, tiled=True)
    w3 = w_all.reshape(n_mp, emb, width)
    x0f = lax.all_to_all(pooled.reshape(n_mp, rows, emb), MP, 0, 0, tiled=True)

    member = members(counts[0], rows)
    cd3 = cross_down.reshape(n_mp, emb, rank)
    cu3 = cross_up.reshape(rank, n_mp, emb)
    bias3 = cross_bias.reshape(n_mp, 1, emb)
    z = jnp.einsum("fcd,fdr->cr", x0f, cd3, preferred_element_type=f32).astype(bf16)
    cross = jnp.einsum("cr,rfd->fcd", z, cu3, preferred_element_type=f32) + bias3
    x1 = (x0f * cross + x0f).astype(bf16)
    act = jnp.einsum("fcd,fdh->ch", x1, w3, preferred_element_type=f32) + tower_bias
    sig = jax.nn.sigmoid(act)
    hidden = (act * sig).astype(bf16)
    pair = dot_last(hidden, user_seg)
    score = jnp.sum(jnp.where(member, pair, 0.0), axis=1) * scale
    dscore = pair_grad(score, member, labels)
    code = jnp.dot(member.astype(bf16), user_seg, preferred_element_type=f32)
    slope = sig * (1.0 + act * (1.0 - sig))
    dact = (dscore[:, None] * code * scale * slope).astype(bf16)
    dx1 = jnp.einsum("ch,fdh->fcd", dact, w3, preferred_element_type=f32)
    dcross = (dx1 * x0f).astype(bf16)
    dz = jnp.einsum("fcd,rfd->cr", dcross, cu3, preferred_element_type=f32).astype(bf16)
    dx0 = dx1 * (1.0 + cross) + jnp.einsum(
        "cr,fdr->fcd", dz, cd3, preferred_element_type=f32
    )
    grads = dx0.astype(bf16)
    returned = lax.all_to_all(grads, MP, 0, 0, tiled=True)
    return (score, returned.reshape(n_mp * rows, 1, emb))


def split_mesh(mesh):
    grid = mesh.devices
    n_dp, n_mp = grid.shape
    try:
        nx = len({d.coords[0] for d in grid[0, :]})
        nc = len({d.core_on_chip for d in grid[:, 0]})
    except AttributeError:
        nx, nc = 1, 1
    if n_mp % nx or n_dp % nc:
        nx, nc = 1, 1
    return Mesh(grid.reshape(n_dp // nc, nc, n_mp // nx, nx), ("y", "c", "z", "x"))


def solution(mesh):
    mesh4 = split_mesh(mesh)
    in_specs = (
        P(MP, None, None),
        P(DP, MP, None),
        P(DP + MP, None),
        P(DP + MP),
        P(),
        P(DP, None),
        P(),
        P(),
        P(),
        P(MP, None),
        P(),
    )
    out_specs = (P(DP + MP), P(DP, MP, None))
    return jax.shard_map(local, mesh=mesh4, in_specs=in_specs, out_specs=out_specs, check_vma=False)
```

```python
import jax
import jax.numpy as jnp
from jax import lax
from jax.experimental import pallas as pl
from jax.experimental.pallas import tpu as pltpu
from jax.sharding import Mesh, PartitionSpec as P


def pool_kernel(ids_ref, tab_ref, out_ref, tabf, acc):
    step = pl.program_id(0)
    blk = out_ref.shape[0]
    total = ids_ref.shape[0] // 2

    @pl.when(step == 0)
    def _():
        tabf[...] = tab_ref[...].astype(jnp.float32)

    base = step * blk

    def body(j, carry):
        for u in range(8):
            c = j * 8 + u
            a = ids_ref[base + c]
            b = ids_ref[total + base + c]
            acc[pl.ds(c, 1), :] = tabf[pl.ds(a, 1), :] + tabf[pl.ds(b, 1), :]
        return carry

    lax.fori_loop(0, blk // 8, body, 0)
    out_ref[...] = acc[...].astype(out_ref.dtype)


def pool_rows(slab, flat_ids, count, blk=1024):
    slab_rows, emb = slab.shape
    spec = pltpu.PrefetchScalarGridSpec(
        num_scalar_prefetch=1,
        grid=(count // blk,),
        in_specs=[pl.BlockSpec((slab_rows, emb), lambda i, ids: (0, 0))],
        out_specs=pl.BlockSpec((blk, emb), lambda i, ids: (i, 0)),
        scratch_shapes=[
            pltpu.VMEM((slab_rows, emb), jnp.float32),
            pltpu.VMEM((blk, emb), jnp.float32),
        ],
    )
    return pl.pallas_call(
        pool_kernel,
        grid_spec=spec,
        out_shape=jax.ShapeDtypeStruct((count, emb), slab.dtype),
    )(flat_ids, slab)


def members(counts_row, rows):
    ends = jnp.cumsum(counts_row)
    starts = ends - counts_row
    place = jnp.arange(rows, dtype=jnp.int32)[:, None]
    return (place >= starts[None, :]) & (place < ends[None, :])


def dot_last(left, right):
    return lax.dot_general(
        left, right, (((1,), (1,)), ((), ())), preferred_element_type=jnp.float32
    )


def pair_grad(scores, member, labels):
    gain = jnp.exp2(labels.astype(jnp.float32))
    member_f = member.astype(jnp.float32)
    same = jnp.dot(member_f, member_f.T) > 0.5
    diff = gain[:, None] - gain[None, :]
    gap = scores[None, :] - scores[:, None]
    turn = jnp.where(diff > 0, jax.nn.sigmoid(gap), jax.nn.sigmoid(-gap))
    total = jnp.sum(jnp.where(same, diff * turn, 0.0), axis=1)
    seg_gain = jnp.sum(jnp.where(member, (gain - 1.0)[:, None], 0.0), axis=0)
    norm = jnp.sum(jnp.where(member, seg_gain[None, :], 0.0), axis=1)
    return -total / jnp.maximum(norm, 1.0)


DP = ("y", "c")
MP = ("z", "x")


def a2a_mp(v, nz, nx):
    shape = v.shape
    v = v.reshape((nz, nx) + shape[1:])
    v = lax.all_to_all(v, "x", split_axis=1, concat_axis=1, tiled=True)
    v = lax.all_to_all(v, "z", split_axis=0, concat_axis=0, tiled=True)
    return v.reshape(shape)


def gather_mp(v, nz, nx):
    v = jnp.broadcast_to(v[None], (nx,) + v.shape)
    v = lax.all_to_all(v, "x", split_axis=0, concat_axis=0, tiled=True)
    v = jnp.broadcast_to(v[None], (nz,) + v.shape)
    v = lax.all_to_all(v, "z", split_axis=0, concat_axis=0, tiled=True)
    return v.reshape((nz * nx,) + v.shape[2:])


def local(
    table,
    ids,
    counts,
    labels,
    request_home,
    user_codes,
    cross_down,
    cross_up,
    cross_bias,
    tower_weight,
    tower_bias,
):
    f32, bf16 = jnp.float32, jnp.bfloat16
    nz, nx = lax.axis_size("z"), lax.axis_size("x")
    n_mp = nz * nx
    n_dp = lax.axis_size("y") * lax.axis_size("c")
    d_idx = lax.axis_index("y") * lax.axis_size("c") + lax.axis_index("c")
    m_idx = lax.axis_index("z") * nx + lax.axis_index("x")
    rows = labels.shape[0]
    seg_count = counts.shape[1]
    width = user_codes.shape[1]
    emb = table.shape[2]
    rank = cross_down.shape[1]
    scale = 1.0 / jnp.sqrt(jnp.float32(width))

    piece = tower_weight.shape[1] // n_dp
    w_piece = lax.dynamic_slice_in_dim(tower_weight, d_idx * piece, piece, axis=1)
    w_grid = lax.all_gather(w_piece, MP + DP, axis=0, tiled=False)
    w_grid = w_grid.reshape((n_mp, n_dp) + w_piece.shape)
    w3 = jnp.transpose(w_grid, (0, 2, 1, 3)).reshape(n_mp, emb, width)

    held = user_codes.shape[0]
    home_local = lax.dynamic_slice_in_dim(request_home, d_idx * held, held)
    wanted = (
        (jnp.arange(n_dp, dtype=jnp.int32)[:, None] * n_mp + m_idx) * seg_count
        + jnp.arange(seg_count, dtype=jnp.int32)[None, :]
    ).reshape(-1)
    pick = (home_local[None, :] == wanted[:, None]).astype(bf16)
    mine = jnp.dot(pick, user_codes, preferred_element_type=f32).astype(bf16)
    sent = lax.all_to_all(mine.reshape(n_dp, seg_count, width), DP, 0, 0, tiled=True)
    user_seg = jnp.sum(sent.astype(f32), axis=0).astype(bf16)

    count = ids.shape[0]
    flat_ids = jnp.transpose(ids[:, 0, :]).reshape(-1)
    pooled = pool_rows(table[0], flat_ids, count)
    x0f = lax.all_to_all(pooled.reshape(n_mp, rows, emb), MP, 0, 0, tiled=True)

    member = members(counts[0], rows)
    cd3 = cross_down.reshape(n_mp, emb, rank)
    cu3 = cross_up.reshape(rank, n_mp, emb)
    bias3 = cross_bias.reshape(n_mp, 1, emb)
    z = jnp.einsum("fcd,fdr->cr", x0f, cd3, preferred_element_type=f32).astype(bf16)
    cross = jnp.einsum("cr,rfd->fcd", z, cu3, preferred_element_type=f32) + bias3
    x1 = (x0f * cross + x0f).astype(bf16)
    act = jnp.einsum("fcd,fdh->ch", x1, w3, preferred_element_type=f32) + tower_bias
    sig = jax.nn.sigmoid(act)
    hidden = (act * sig).astype(bf16)
    pair = dot_last(hidden, user_seg)
    score = jnp.sum(jnp.where(member, pair, 0.0), axis=1) * scale
    dscore = pair_grad(score, member, labels)
    code = jnp.dot(member.astype(bf16), user_seg, preferred_element_type=f32)
    slope = sig * (1.0 + act * (1.0 - sig))
    dact = (dscore[:, None] * code * scale * slope).astype(bf16)
    dx1 = jnp.einsum("ch,fdh->fcd", dact, w3, preferred_element_type=f32)
    dcross = (dx1 * x0f).astype(bf16)
    dz = jnp.einsum("fcd,rfd->cr", dcross, cu3, preferred_element_type=f32).astype(bf16)
    dx0 = dx1 * (1.0 + cross) + jnp.einsum(
        "cr,fdr->fcd", dz, cd3, preferred_element_type=f32
    )
    grads = dx0.astype(bf16)
    returned = lax.all_to_all(grads, MP, 0, 0, tiled=True)
    return (score, returned.reshape(n_mp * rows, 1, emb))


def split_mesh(mesh):
    grid = mesh.devices
    n_dp, n_mp = grid.shape
    try:
        nx = len({d.coords[0] for d in grid[0, :]})
        nc = len({d.core_on_chip for d in grid[:, 0]})
    except AttributeError:
        nx, nc = 1, 1
    if n_mp % nx or n_dp % nc:
        nx, nc = 1, 1
    return Mesh(grid.reshape(n_dp // nc, nc, n_mp // nx, nx), ("y", "c", "z", "x"))


def solution(mesh):
    mesh4 = split_mesh(mesh)
    in_specs = (
        P(MP, None, None),
        P(DP, MP, None),
        P(DP + MP, None),
        P(DP + MP),
        P(),
        P(DP, None),
        P(),
        P(),
        P(),
        P(MP, None),
        P(),
    )
    out_specs = (P(DP + MP), P(DP, MP, None))
    return jax.shard_map(local, mesh=mesh4, in_specs=in_specs, out_specs=out_specs, check_vma=False)
```

```python
import jax
import jax.numpy as jnp
from jax import lax
from jax.experimental import pallas as pl
from jax.experimental.pallas import tpu as pltpu
from jax.sharding import Mesh, PartitionSpec as P


def pool_kernel(ids_ref, tab_ref, out_ref, tabf, acc):
    step = pl.program_id(0)
    blk = out_ref.shape[0]
    total = ids_ref.shape[0] // 2

    @pl.when(step == 0)
    def _():
        tabf[...] = tab_ref[...].astype(jnp.float32)

    base = step * blk

    def body(j, carry):
        for u in range(8):
            c = j * 8 + u
            a = ids_ref[base + c]
            b = ids_ref[total + base + c]
            acc[pl.ds(c, 1), :] = tabf[pl.ds(a, 1), :] + tabf[pl.ds(b, 1), :]
        return carry

    lax.fori_loop(0, blk // 8, body, 0)
    out_ref[...] = acc[...].astype(out_ref.dtype)


def pool_rows(slab, flat_ids, count, blk=1024):
    slab_rows, emb = slab.shape
    spec = pltpu.PrefetchScalarGridSpec(
        num_scalar_prefetch=1,
        grid=(count // blk,),
        in_specs=[pl.BlockSpec((slab_rows, emb), lambda i, ids: (0, 0))],
        out_specs=pl.BlockSpec((blk, emb), lambda i, ids: (i, 0)),
        scratch_shapes=[
            pltpu.VMEM((slab_rows, emb), jnp.float32),
            pltpu.VMEM((blk, emb), jnp.float32),
        ],
    )
    return pl.pallas_call(
        pool_kernel,
        grid_spec=spec,
        out_shape=jax.ShapeDtypeStruct((count, emb), slab.dtype),
    )(flat_ids, slab)


def members(counts_row, rows):
    ends = jnp.cumsum(counts_row)
    starts = ends - counts_row
    place = jnp.arange(rows, dtype=jnp.int32)[:, None]
    return (place >= starts[None, :]) & (place < ends[None, :])


def dot_last(left, right):
    return lax.dot_general(
        left, right, (((1,), (1,)), ((), ())), preferred_element_type=jnp.float32
    )


def pair_grad(scores, member, labels):
    gain = jnp.exp2(labels.astype(jnp.float32))
    member_f = member.astype(jnp.float32)
    same = jnp.dot(member_f, member_f.T) > 0.5
    diff = gain[:, None] - gain[None, :]
    gap = scores[None, :] - scores[:, None]
    turn = jnp.where(diff > 0, jax.nn.sigmoid(gap), jax.nn.sigmoid(-gap))
    total = jnp.sum(jnp.where(same, diff * turn, 0.0), axis=1)
    seg_gain = jnp.sum(jnp.where(member, (gain - 1.0)[:, None], 0.0), axis=0)
    norm = jnp.sum(jnp.where(member, seg_gain[None, :], 0.0), axis=1)
    return -total / jnp.maximum(norm, 1.0)


DP = ("y", "c")
MP = ("z", "x")


def local(
    table,
    ids,
    counts,
    labels,
    request_home,
    user_codes,
    cross_down,
    cross_up,
    cross_bias,
    tower_weight,
    tower_bias,
):
    f32, bf16 = jnp.float32, jnp.bfloat16
    nz, nx = lax.axis_size("z"), lax.axis_size("x")
    n_mp = nz * nx
    n_dp = lax.axis_size("y") * lax.axis_size("c")
    d_idx = lax.axis_index("y") * lax.axis_size("c") + lax.axis_index("c")
    m_idx = lax.axis_index("z") * nx + lax.axis_index("x")
    rows = labels.shape[0]
    seg_count = counts.shape[1]
    width = user_codes.shape[1]
    emb = table.shape[2]
    rank = cross_down.shape[1]
    scale = 1.0 / jnp.sqrt(jnp.float32(width))

    piece = tower_weight.shape[1] // n_dp
    w_piece = lax.dynamic_slice_in_dim(tower_weight, d_idx * piece, piece, axis=1)
    w_cols = lax.all_to_all(
        jnp.broadcast_to(w_piece[None], (n_mp,) + w_piece.shape), MP, 0, 0, tiled=True
    ).reshape(n_mp * w_piece.shape[0], piece)

    held = user_codes.shape[0]
    home_local = lax.dynamic_slice_in_dim(request_home, d_idx * held, held)
    wanted = (
        (jnp.arange(n_dp, dtype=jnp.int32)[:, None] * n_mp + m_idx) * seg_count
        + jnp.arange(seg_count, dtype=jnp.int32)[None, :]
    ).reshape(-1)
    pick = (home_local[None, :] == wanted[:, None]).astype(bf16)
    mine = jnp.dot(pick, user_codes, preferred_element_type=f32).astype(bf16)
    user_seg = lax.psum_scatter(
        mine.reshape(n_dp, seg_count, width), DP, scatter_dimension=0, tiled=False
    )

    count = ids.shape[0]
    flat_ids = jnp.transpose(ids[:, 0, :]).reshape(-1)
    pooled = pool_rows(table[0], flat_ids, count)
    w_cols, pooled = lax.optimization_barrier((w_cols, pooled))
    w_all = lax.all_gather(w_cols, DP, axis=1, tiled=True)
    w3 = w_all.reshape(n_mp, emb, width)
    x0f = lax.all_to_all(pooled.reshape(n_mp, rows, emb), MP, 0, 0, tiled=True)

    member = members(counts[0], rows)
    cd3 = cross_down.reshape(n_mp, emb, rank)
    cu3 = cross_up.reshape(rank, n_mp, emb)
    bias3 = cross_bias.reshape(n_mp, 1, emb)
    z = jnp.einsum("fcd,fdr->cr", x0f, cd3, preferred_element_type=f32).astype(bf16)
    cross = jnp.einsum("cr,rfd->fcd", z, cu3, preferred_element_type=f32) + bias3
    x1 = (x0f * cross + x0f).astype(bf16)
    act = jnp.einsum("fcd,fdh->ch", x1, w3, preferred_element_type=f32) + tower_bias
    sig = jax.nn.sigmoid(act)
    hidden = (act * sig).astype(bf16)
    pair = dot_last(hidden, user_seg)
    score = jnp.sum(jnp.where(member, pair, 0.0), axis=1) * scale
    dscore = pair_grad(score, member, labels)
    code = jnp.dot(member.astype(bf16), user_seg, preferred_element_type=f32)
    slope = sig * (1.0 + act * (1.0 - sig))
    dact = (dscore[:, None] * code * scale * slope).astype(bf16)
    dx1 = jnp.einsum("ch,fdh->fcd", dact, w3, preferred_element_type=f32)
    dcross = (dx1 * x0f).astype(bf16)
    dz = jnp.einsum("fcd,rfd->cr", dcross, cu3, preferred_element_type=f32).astype(bf16)
    dx0 = dx1 * (1.0 + cross) + jnp.einsum(
        "cr,fdr->fcd", dz, cd3, preferred_element_type=f32
    )
    grads = dx0.astype(bf16)
    returned = lax.all_to_all(grads, MP, 0, 0, tiled=True)
    return (score, returned.reshape(n_mp * rows, 1, emb))


def split_mesh(mesh):
    grid = mesh.devices
    n_dp, n_mp = grid.shape
    try:
        nx = len({d.coords[0] for d in grid[0, :]})
        nc = len({d.core_on_chip for d in grid[:, 0]})
    except AttributeError:
        nx, nc = 1, 1
    if n_mp % nx or n_dp % nc:
        nx, nc = 1, 1
    return Mesh(grid.reshape(n_dp // nc, nc, n_mp // nx, nx), ("y", "c", "z", "x"))


def solution(mesh):
    mesh4 = split_mesh(mesh)
    in_specs = (
        P(MP, None, None),
        P(DP, MP, None),
        P(DP + MP, None),
        P(DP + MP),
        P(),
        P(DP, None),
        P(),
        P(),
        P(),
        P(MP, None),
        P(),
    )
    out_specs = (P(DP + MP), P(DP, MP, None))
    return jax.shard_map(local, mesh=mesh4, in_specs=in_specs, out_specs=out_specs, check_vma=False)
```

```python
import jax
import jax.numpy as jnp
from jax import lax
from jax.experimental import pallas as pl
from jax.experimental.pallas import tpu as pltpu
from jax.sharding import Mesh, PartitionSpec as P


def pool_kernel(ids_ref, tab_ref, out_ref, tabf, acc):
    step = pl.program_id(0)
    blk = out_ref.shape[0]
    total = ids_ref.shape[0] // 2

    @pl.when(step == 0)
    def _():
        tabf[...] = tab_ref[...].astype(jnp.float32)

    base = step * blk

    def body(j, carry):
        for u in range(8):
            c = j * 8 + u
            a = ids_ref[base + c]
            b = ids_ref[total + base + c]
            acc[pl.ds(c, 1), :] = tabf[pl.ds(a, 1), :] + tabf[pl.ds(b, 1), :]
        return carry

    lax.fori_loop(0, blk // 8, body, 0)
    out_ref[...] = acc[...].astype(out_ref.dtype)


def pool_rows(slab, flat_ids, count, blk=1024):
    slab_rows, emb = slab.shape
    spec = pltpu.PrefetchScalarGridSpec(
        num_scalar_prefetch=1,
        grid=(count // blk,),
        in_specs=[pl.BlockSpec((slab_rows, emb), lambda i, ids: (0, 0))],
        out_specs=pl.BlockSpec((blk, emb), lambda i, ids: (i, 0)),
        scratch_shapes=[
            pltpu.VMEM((slab_rows, emb), jnp.float32),
            pltpu.VMEM((blk, emb), jnp.float32),
        ],
    )
    return pl.pallas_call(
        pool_kernel,
        grid_spec=spec,
        out_shape=jax.ShapeDtypeStruct((count, emb), slab.dtype),
    )(flat_ids, slab)


def members(counts_row, rows):
    ends = jnp.cumsum(counts_row)
    starts = ends - counts_row
    place = jnp.arange(rows, dtype=jnp.int32)[:, None]
    return (place >= starts[None, :]) & (place < ends[None, :])


def dot_last(left, right):
    return lax.dot_general(
        left, right, (((1,), (1,)), ((), ())), preferred_element_type=jnp.float32
    )


def pair_grad(scores, member, labels):
    gain = jnp.exp2(labels.astype(jnp.float32))
    member_f = member.astype(jnp.float32)
    same = jnp.dot(member_f, member_f.T) > 0.5
    diff = gain[:, None] - gain[None, :]
    gap = scores[None, :] - scores[:, None]
    turn = jnp.where(diff > 0, jax.nn.sigmoid(gap), jax.nn.sigmoid(-gap))
    total = jnp.sum(jnp.where(same, diff * turn, 0.0), axis=1)
    seg_gain = jnp.sum(jnp.where(member, (gain - 1.0)[:, None], 0.0), axis=0)
    norm = jnp.sum(jnp.where(member, seg_gain[None, :], 0.0), axis=1)
    return -total / jnp.maximum(norm, 1.0)


DP = ("y", "c")
MP = ("z", "x")


def local(
    table,
    ids,
    counts,
    labels,
    request_home,
    user_codes,
    cross_down,
    cross_up,
    cross_bias,
    tower_weight,
    tower_bias,
):
    f32, bf16 = jnp.float32, jnp.bfloat16
    nz, nx = lax.axis_size("z"), lax.axis_size("x")
    n_mp = nz * nx
    n_dp = lax.axis_size("y") * lax.axis_size("c")
    d_idx = lax.axis_index("y") * lax.axis_size("c") + lax.axis_index("c")
    m_idx = lax.axis_index("z") * nx + lax.axis_index("x")
    rows = labels.shape[0]
    seg_count = counts.shape[1]
    width = user_codes.shape[1]
    emb = table.shape[2]
    rank = cross_down.shape[1]
    scale = 1.0 / jnp.sqrt(jnp.float32(width))

    piece = tower_weight.shape[1] // n_dp
    w_piece = lax.dynamic_slice_in_dim(tower_weight, d_idx * piece, piece, axis=1)
    w_cols = lax.all_to_all(
        jnp.broadcast_to(w_piece[None], (n_mp,) + w_piece.shape), MP, 0, 0, tiled=True
    ).reshape(n_mp * w_piece.shape[0], piece)

    held = user_codes.shape[0]
    home_local = lax.dynamic_slice_in_dim(request_home, d_idx * held, held)
    wanted = (
        (jnp.arange(n_dp, dtype=jnp.int32)[:, None] * n_mp + m_idx) * seg_count
        + jnp.arange(seg_count, dtype=jnp.int32)[None, :]
    ).reshape(-1)
    pick = (home_local[None, :] == wanted[:, None]).astype(bf16)
    mine = jnp.dot(pick, user_codes, preferred_element_type=f32).astype(bf16)

    count = ids.shape[0]
    flat_ids = jnp.transpose(ids[:, 0, :]).reshape(-1)
    pooled = pool_rows(table[0], flat_ids, count)
    w_cols, pooled = lax.optimization_barrier((w_cols, pooled))
    payload = jnp.concatenate([w_cols, mine.reshape(-1, piece)], axis=0)
    both = lax.all_gather(payload, DP, axis=1, tiled=True)
    w3 = both[: w_cols.shape[0]].reshape(n_mp, emb, width)
    ride = seg_count * width // piece
    mine_all = lax.dynamic_slice_in_dim(both, w_cols.shape[0] + d_idx * ride, ride, axis=0)
    mine_all = mine_all.reshape(seg_count, width // piece, n_dp, piece)
    user_seg = jnp.sum(mine_all.astype(f32), axis=2).reshape(seg_count, width).astype(bf16)
    x0f = lax.all_to_all(pooled.reshape(n_mp, rows, emb), MP, 0, 0, tiled=True)

    member = members(counts[0], rows)
    cd3 = cross_down.reshape(n_mp, emb, rank)
    cu3 = cross_up.reshape(rank, n_mp, emb)
    bias3 = cross_bias.reshape(n_mp, 1, emb)
    z = jnp.einsum("fcd,fdr->cr", x0f, cd3, preferred_element_type=f32).astype(bf16)
    cross = jnp.einsum("cr,rfd->fcd", z, cu3, preferred_element_type=f32) + bias3
    x1 = (x0f * cross + x0f).astype(bf16)
    act = jnp.einsum("fcd,fdh->ch", x1, w3, preferred_element_type=f32) + tower_bias
    sig = jax.nn.sigmoid(act)
    hidden = (act * sig).astype(bf16)
    pair = dot_last(hidden, user_seg)
    score = jnp.sum(jnp.where(member, pair, 0.0), axis=1) * scale
    dscore = pair_grad(score, member, labels)
    code = jnp.dot(member.astype(bf16), user_seg, preferred_element_type=f32)
    slope = sig * (1.0 + act * (1.0 - sig))
    dact = (dscore[:, None] * code * scale * slope).astype(bf16)
    dx1 = jnp.einsum("ch,fdh->fcd", dact, w3, preferred_element_type=f32)
    dcross = (dx1 * x0f).astype(bf16)
    dz = jnp.einsum("fcd,rfd->cr", dcross, cu3, preferred_element_type=f32).astype(bf16)
    dx0 = dx1 * (1.0 + cross) + jnp.einsum(
        "cr,fdr->fcd", dz, cd3, preferred_element_type=f32
    )
    grads = dx0.astype(bf16)
    returned = lax.all_to_all(grads, MP, 0, 0, tiled=True)
    return (score, returned.reshape(n_mp * rows, 1, emb))


def split_mesh(mesh):
    grid = mesh.devices
    n_dp, n_mp = grid.shape
    try:
        nx = len({d.coords[0] for d in grid[0, :]})
        nc = len({d.core_on_chip for d in grid[:, 0]})
    except AttributeError:
        nx, nc = 1, 1
    if n_mp % nx or n_dp % nc:
        nx, nc = 1, 1
    return Mesh(grid.reshape(n_dp // nc, nc, n_mp // nx, nx), ("y", "c", "z", "x"))


def solution(mesh):
    mesh4 = split_mesh(mesh)
    in_specs = (
        P(MP, None, None),
        P(DP, MP, None),
        P(DP + MP, None),
        P(DP + MP),
        P(),
        P(DP, None),
        P(),
        P(),
        P(),
        P(MP, None),
        P(),
    )
    out_specs = (P(DP + MP), P(DP, MP, None))
    return jax.shard_map(local, mesh=mesh4, in_specs=in_specs, out_specs=out_specs, check_vma=False)
```

```python
import jax
import jax.numpy as jnp
from jax import lax
from jax.experimental import pallas as pl
from jax.experimental.pallas import tpu as pltpu
from jax.sharding import Mesh, PartitionSpec as P


def pool_kernel(ids_ref, tab_ref, out_ref, tabf, acc):
    step = pl.program_id(0)
    blk = out_ref.shape[0]
    total = ids_ref.shape[0] // 2

    @pl.when(step == 0)
    def _():
        tabf[...] = tab_ref[...].astype(jnp.float32)

    base = step * blk

    def body(j, carry):
        for u in range(8):
            c = j * 8 + u
            a = ids_ref[base + c]
            b = ids_ref[total + base + c]
            acc[pl.ds(c, 1), :] = tabf[pl.ds(a, 1), :] + tabf[pl.ds(b, 1), :]
        return carry

    lax.fori_loop(0, blk // 8, body, 0)
    out_ref[...] = acc[...].astype(out_ref.dtype)


def pool_rows(slab, flat_ids, count, blk=1024):
    slab_rows, emb = slab.shape
    spec = pltpu.PrefetchScalarGridSpec(
        num_scalar_prefetch=1,
        grid=(count // blk,),
        in_specs=[pl.BlockSpec((slab_rows, emb), lambda i, ids: (0, 0))],
        out_specs=pl.BlockSpec((blk, emb), lambda i, ids: (i, 0)),
        scratch_shapes=[
            pltpu.VMEM((slab_rows, emb), jnp.float32),
            pltpu.VMEM((blk, emb), jnp.float32),
        ],
    )
    return pl.pallas_call(
        pool_kernel,
        grid_spec=spec,
        out_shape=jax.ShapeDtypeStruct((count, emb), slab.dtype),
    )(flat_ids, slab)


def members(counts_row, rows):
    ends = jnp.cumsum(counts_row)
    starts = ends - counts_row
    place = jnp.arange(rows, dtype=jnp.int32)[:, None]
    return (place >= starts[None, :]) & (place < ends[None, :])


def dot_last(left, right):
    return lax.dot_general(
        left, right, (((1,), (1,)), ((), ())), preferred_element_type=jnp.float32
    )


def pair_grad(scores, member, labels):
    gain = jnp.exp2(labels.astype(jnp.float32))
    member_f = member.astype(jnp.float32)
    same = jnp.dot(member_f, member_f.T) > 0.5
    diff = gain[:, None] - gain[None, :]
    gap = scores[None, :] - scores[:, None]
    turn = jnp.where(diff > 0, jax.nn.sigmoid(gap), jax.nn.sigmoid(-gap))
    total = jnp.sum(jnp.where(same, diff * turn, 0.0), axis=1)
    seg_gain = jnp.sum(jnp.where(member, (gain - 1.0)[:, None], 0.0), axis=0)
    norm = jnp.sum(jnp.where(member, seg_gain[None, :], 0.0), axis=1)
    return -total / jnp.maximum(norm, 1.0)


DP = ("y", "c")
MP = ("z", "x")


def local(
    table,
    ids,
    counts,
    labels,
    request_home,
    user_codes,
    cross_down,
    cross_up,
    cross_bias,
    tower_weight,
    tower_bias,
):
    f32, bf16 = jnp.float32, jnp.bfloat16
    nz, nx = lax.axis_size("z"), lax.axis_size("x")
    n_mp = nz * nx
    n_dp = lax.axis_size("y") * lax.axis_size("c")
    d_idx = lax.axis_index("y") * lax.axis_size("c") + lax.axis_index("c")
    m_idx = lax.axis_index("z") * nx + lax.axis_index("x")
    rows = labels.shape[0]
    seg_count = counts.shape[1]
    width = user_codes.shape[1]
    emb = table.shape[2]
    rank = cross_down.shape[1]
    scale = 1.0 / jnp.sqrt(jnp.float32(width))

    piece = tower_weight.shape[1] // n_dp
    w_piece = lax.dynamic_slice_in_dim(tower_weight, d_idx * piece, piece, axis=1)
    w_cols = lax.all_to_all(
        jnp.broadcast_to(w_piece[None], (n_mp,) + w_piece.shape), MP, 0, 0, tiled=True
    ).reshape(n_mp * w_piece.shape[0], piece)

    held = user_codes.shape[0]
    home_local = lax.dynamic_slice_in_dim(request_home, d_idx * held, held)
    wanted = (
        (jnp.arange(n_dp, dtype=jnp.int32)[:, None] * n_mp + m_idx) * seg_count
        + jnp.arange(seg_count, dtype=jnp.int32)[None, :]
    ).reshape(-1)
    pick = (home_local[None, :] == wanted[:, None]).astype(bf16)
    mine = jnp.dot(pick, user_codes, preferred_element_type=f32).astype(bf16)

    count = ids.shape[0]
    flat_ids = jnp.transpose(ids[:, 0, :]).reshape(-1)
    pooled = pool_rows(table[0], flat_ids, count)
    w_cols, pooled = lax.optimization_barrier((w_cols, pooled))
    payload = jnp.concatenate([w_cols, mine.reshape(-1, piece)], axis=0)
    both = lax.all_gather(payload, DP, axis=1, tiled=True)
    w3 = both.reshape(-1, emb, width)
    extra = w3.shape[0] - n_mp
    ride = seg_count * width // piece
    mine_all = lax.dynamic_slice_in_dim(both, w_cols.shape[0] + d_idx * ride, ride, axis=0)
    mine_all = mine_all.reshape(seg_count, width // piece, n_dp, piece)
    user_seg = jnp.sum(mine_all.astype(f32), axis=2).reshape(seg_count, width).astype(bf16)
    x0f = lax.all_to_all(pooled.reshape(n_mp, rows, emb), MP, 0, 0, tiled=True)

    member = members(counts[0], rows)
    cd3 = cross_down.reshape(n_mp, emb, rank)
    cu3 = cross_up.reshape(rank, n_mp, emb)
    bias3 = cross_bias.reshape(n_mp, 1, emb)
    z = jnp.einsum("fcd,fdr->cr", x0f, cd3, preferred_element_type=f32).astype(bf16)
    cross = jnp.einsum("cr,rfd->fcd", z, cu3, preferred_element_type=f32) + bias3
    x1 = (x0f * cross + x0f).astype(bf16)
    x1p = jnp.pad(x1, ((0, extra), (0, 0), (0, 0)))
    act = jnp.einsum("fcd,fdh->ch", x1p, w3, preferred_element_type=f32) + tower_bias
    sig = jax.nn.sigmoid(act)
    hidden = (act * sig).astype(bf16)
    pair = dot_last(hidden, user_seg)
    score = jnp.sum(jnp.where(member, pair, 0.0), axis=1) * scale
    dscore = pair_grad(score, member, labels)
    code = jnp.dot(member.astype(bf16), user_seg, preferred_element_type=f32)
    slope = sig * (1.0 + act * (1.0 - sig))
    dact = (dscore[:, None] * code * scale * slope).astype(bf16)
    dx1 = jnp.einsum("ch,fdh->fcd", dact, w3, preferred_element_type=f32)[:n_mp]
    dcross = (dx1 * x0f).astype(bf16)
    dz = jnp.einsum("fcd,rfd->cr", dcross, cu3, preferred_element_type=f32).astype(bf16)
    dx0 = dx1 * (1.0 + cross) + jnp.einsum(
        "cr,fdr->fcd", dz, cd3, preferred_element_type=f32
    )
    grads = dx0.astype(bf16)
    returned = lax.all_to_all(grads, MP, 0, 0, tiled=True)
    return (score, returned.reshape(n_mp * rows, 1, emb))


def split_mesh(mesh):
    grid = mesh.devices
    n_dp, n_mp = grid.shape
    try:
        nx = len({d.coords[0] for d in grid[0, :]})
        nc = len({d.core_on_chip for d in grid[:, 0]})
    except AttributeError:
        nx, nc = 1, 1
    if n_mp % nx or n_dp % nc:
        nx, nc = 1, 1
    return Mesh(grid.reshape(n_dp // nc, nc, n_mp // nx, nx), ("y", "c", "z", "x"))


def solution(mesh):
    mesh4 = split_mesh(mesh)
    in_specs = (
        P(MP, None, None),
        P(DP, MP, None),
        P(DP + MP, None),
        P(DP + MP),
        P(),
        P(DP, None),
        P(),
        P(),
        P(),
        P(MP, None),
        P(),
    )
    out_specs = (P(DP + MP), P(DP, MP, None))
    return jax.shard_map(local, mesh=mesh4, in_specs=in_specs, out_specs=out_specs, check_vma=False)
```

```python
import jax
import jax.numpy as jnp
from jax import lax
from jax.experimental import pallas as pl
from jax.experimental.pallas import tpu as pltpu
from jax.sharding import Mesh, PartitionSpec as P


def pool_kernel(ids_ref, tab_ref, out_ref, tabf, acc):
    step = pl.program_id(0)
    blk = out_ref.shape[0]
    total = ids_ref.shape[0] // 2

    @pl.when(step == 0)
    def _():
        tabf[...] = tab_ref[...].astype(jnp.float32)

    base = step * blk

    def body(j, carry):
        for u in range(8):
            c = j * 8 + u
            a = ids_ref[base + c]
            b = ids_ref[total + base + c]
            acc[pl.ds(c, 1), :] = tabf[pl.ds(a, 1), :] + tabf[pl.ds(b, 1), :]
        return carry

    lax.fori_loop(0, blk // 8, body, 0)
    out_ref[...] = acc[...].astype(out_ref.dtype)


def pool_rows(slab, flat_ids, count, blk=1024):
    slab_rows, emb = slab.shape
    spec = pltpu.PrefetchScalarGridSpec(
        num_scalar_prefetch=1,
        grid=(count // blk,),
        in_specs=[pl.BlockSpec((slab_rows, emb), lambda i, ids: (0, 0))],
        out_specs=pl.BlockSpec((blk, emb), lambda i, ids: (i, 0)),
        scratch_shapes=[
            pltpu.VMEM((slab_rows, emb), jnp.float32),
            pltpu.VMEM((blk, emb), jnp.float32),
        ],
    )
    return pl.pallas_call(
        pool_kernel,
        grid_spec=spec,
        out_shape=jax.ShapeDtypeStruct((count, emb), slab.dtype),
    )(flat_ids, slab)


def members(counts_row, rows):
    ends = jnp.cumsum(counts_row)
    starts = ends - counts_row
    place = jnp.arange(rows, dtype=jnp.int32)[:, None]
    return (place >= starts[None, :]) & (place < ends[None, :])


def dot_last(left, right):
    return lax.dot_general(
        left, right, (((1,), (1,)), ((), ())), preferred_element_type=jnp.float32
    )


def pair_grad(scores, member, labels):
    gain = jnp.exp2(labels.astype(jnp.float32))
    member_f = member.astype(jnp.float32)
    same = jnp.dot(member_f, member_f.T) > 0.5
    diff = gain[:, None] - gain[None, :]
    gap = scores[None, :] - scores[:, None]
    turn = jnp.where(diff > 0, jax.nn.sigmoid(gap), jax.nn.sigmoid(-gap))
    total = jnp.sum(jnp.where(same, diff * turn, 0.0), axis=1)
    seg_gain = jnp.sum(jnp.where(member, (gain - 1.0)[:, None], 0.0), axis=0)
    norm = jnp.sum(jnp.where(member, seg_gain[None, :], 0.0), axis=1)
    return -total / jnp.maximum(norm, 1.0)


DP = ("y", "c")
MP = ("z", "x")


def local(
    table,
    ids,
    counts,
    labels,
    request_home,
    user_codes,
    cross_down,
    cross_up,
    cross_bias,
    tower_weight,
    tower_bias,
):
    f32, bf16 = jnp.float32, jnp.bfloat16
    nz, nx = lax.axis_size("z"), lax.axis_size("x")
    n_mp = nz * nx
    n_dp = lax.axis_size("y") * lax.axis_size("c")
    d_idx = lax.axis_index("y") * lax.axis_size("c") + lax.axis_index("c")
    m_idx = lax.axis_index("z") * nx + lax.axis_index("x")
    rows = labels.shape[0]
    seg_count = counts.shape[1]
    width = user_codes.shape[1]
    emb = table.shape[2]
    rank = cross_down.shape[1]
    scale = 1.0 / jnp.sqrt(jnp.float32(width))

    piece = tower_weight.shape[1] // n_dp
    w_piece = lax.dynamic_slice_in_dim(tower_weight, d_idx * piece, piece, axis=1)
    w_cols = lax.all_to_all(
        jnp.broadcast_to(w_piece[None], (n_mp,) + w_piece.shape), MP, 0, 0, tiled=True
    ).reshape(n_mp * w_piece.shape[0], piece)

    held = user_codes.shape[0]
    home_local = lax.dynamic_slice_in_dim(request_home, d_idx * held, held)
    wanted = (
        (jnp.arange(n_dp, dtype=jnp.int32)[:, None] * n_mp + m_idx) * seg_count
        + jnp.arange(seg_count, dtype=jnp.int32)[None, :]
    ).reshape(-1)
    pick = (home_local[None, :] == wanted[:, None]).astype(bf16)
    mine = jnp.dot(pick, user_codes, preferred_element_type=f32).astype(bf16)

    count = ids.shape[0]
    flat_ids = jnp.transpose(ids[:, 0, :]).reshape(-1)
    pooled = pool_rows(table[0], flat_ids, count)
    w_cols, pooled = lax.optimization_barrier((w_cols, pooled))
    w_all, mine_all = lax.all_gather((w_cols, mine.reshape(-1, piece)), DP, axis=1, tiled=True)
    w3 = w_all.reshape(n_mp, emb, width)
    ride = seg_count * width // piece
    mine_all = lax.dynamic_slice_in_dim(mine_all, d_idx * ride, ride, axis=0)
    mine_all = mine_all.reshape(seg_count, width // piece, n_dp, piece)
    user_seg = jnp.sum(mine_all.astype(f32), axis=2).reshape(seg_count, width).astype(bf16)
    x0f = lax.all_to_all(pooled.reshape(n_mp, rows, emb), MP, 0, 0, tiled=True)

    member = members(counts[0], rows)
    cd3 = cross_down.reshape(n_mp, emb, rank)
    cu3 = cross_up.reshape(rank, n_mp, emb)
    bias3 = cross_bias.reshape(n_mp, 1, emb)
    z = jnp.einsum("fcd,fdr->cr", x0f, cd3, preferred_element_type=f32).astype(bf16)
    cross = jnp.einsum("cr,rfd->fcd", z, cu3, preferred_element_type=f32) + bias3
    x1 = (x0f * cross + x0f).astype(bf16)
    act = jnp.einsum("fcd,fdh->ch", x1, w3, preferred_element_type=f32) + tower_bias
    sig = jax.nn.sigmoid(act)
    hidden = (act * sig).astype(bf16)
    pair = dot_last(hidden, user_seg)
    score = jnp.sum(jnp.where(member, pair, 0.0), axis=1) * scale
    dscore = pair_grad(score, member, labels)
    code = jnp.dot(member.astype(bf16), user_seg, preferred_element_type=f32)
    slope = sig * (1.0 + act * (1.0 - sig))
    dact = (dscore[:, None] * code * scale * slope).astype(bf16)
    dx1 = jnp.einsum("ch,fdh->fcd", dact, w3, preferred_element_type=f32)
    dcross = (dx1 * x0f).astype(bf16)
    dz = jnp.einsum("fcd,rfd->cr", dcross, cu3, preferred_element_type=f32).astype(bf16)
    dx0 = dx1 * (1.0 + cross) + jnp.einsum(
        "cr,fdr->fcd", dz, cd3, preferred_element_type=f32
    )
    grads = dx0.astype(bf16)
    returned = lax.all_to_all(grads, MP, 0, 0, tiled=True)
    return (score, returned.reshape(n_mp * rows, 1, emb))


def split_mesh(mesh):
    grid = mesh.devices
    n_dp, n_mp = grid.shape
    try:
        nx = len({d.coords[0] for d in grid[0, :]})
        nc = len({d.core_on_chip for d in grid[:, 0]})
    except AttributeError:
        nx, nc = 1, 1
    if n_mp % nx or n_dp % nc:
        nx, nc = 1, 1
    return Mesh(grid.reshape(n_dp // nc, nc, n_mp // nx, nx), ("y", "c", "z", "x"))


def solution(mesh):
    mesh4 = split_mesh(mesh)
    in_specs = (
        P(MP, None, None),
        P(DP, MP, None),
        P(DP + MP, None),
        P(DP + MP),
        P(),
        P(DP, None),
        P(),
        P(),
        P(),
        P(MP, None),
        P(),
    )
    out_specs = (P(DP + MP), P(DP, MP, None))
    return jax.shard_map(local, mesh=mesh4, in_specs=in_specs, out_specs=out_specs, check_vma=False)
```

```python
import jax
import jax.numpy as jnp
from jax import lax
from jax.experimental import pallas as pl
from jax.experimental.pallas import tpu as pltpu
from jax.sharding import Mesh, PartitionSpec as P


def pool_kernel(ids_ref, tab_ref, out_ref, tabf, acc):
    step = pl.program_id(0)
    blk = out_ref.shape[0]
    total = ids_ref.shape[0] // 2

    @pl.when(step == 0)
    def _():
        tabf[...] = tab_ref[...].astype(jnp.float32)

    base = step * blk

    def body(j, carry):
        for u in range(8):
            c = j * 8 + u
            a = ids_ref[base + c]
            b = ids_ref[total + base + c]
            acc[pl.ds(c, 1), :] = tabf[pl.ds(a, 1), :] + tabf[pl.ds(b, 1), :]
        return carry

    lax.fori_loop(0, blk // 8, body, 0)
    out_ref[...] = acc[...].astype(out_ref.dtype)


def pool_rows(slab, flat_ids, count, blk=1024):
    slab_rows, emb = slab.shape
    spec = pltpu.PrefetchScalarGridSpec(
        num_scalar_prefetch=1,
        grid=(count // blk,),
        in_specs=[pl.BlockSpec((slab_rows, emb), lambda i, ids: (0, 0))],
        out_specs=pl.BlockSpec((blk, emb), lambda i, ids: (i, 0)),
        scratch_shapes=[
            pltpu.VMEM((slab_rows, emb), jnp.float32),
            pltpu.VMEM((blk, emb), jnp.float32),
        ],
    )
    return pl.pallas_call(
        pool_kernel,
        grid_spec=spec,
        out_shape=jax.ShapeDtypeStruct((count, emb), slab.dtype),
    )(flat_ids, slab)


def back_kernel(dx1_ref, x0_ref, cross_ref, up_ref, down_ref, out_ref):
    feats, _, emb = dx1_ref.shape
    contract = (((1,), (1,)), ((), ()))

    def down_pass(f, acc):
        cols = pl.ds(pl.multiple_of(f * emb, emb), emb)
        dcross = (dx1_ref[f] * x0_ref[f].astype(jnp.float32)).astype(jnp.bfloat16)
        return acc + lax.dot_general(
            dcross, up_ref[:, cols], contract, preferred_element_type=jnp.float32
        )

    acc = jnp.zeros((dx1_ref.shape[1], up_ref.shape[0]), jnp.float32)
    dz = lax.fori_loop(0, feats, down_pass, acc).astype(jnp.bfloat16)

    def up_pass(f, carry):
        rows = pl.ds(pl.multiple_of(f * emb, emb), emb)
        back = lax.dot_general(
            dz, down_ref[rows, :], contract, preferred_element_type=jnp.float32
        )
        out_ref[f] = (dx1_ref[f] * (1.0 + cross_ref[f]) + back).astype(out_ref.dtype)
        return carry

    lax.fori_loop(0, feats, up_pass, 0)


def back_rows(dx1, x0f, cross, cross_up, cross_down, blk=128):
    feats, rows, emb = dx1.shape
    part = pl.BlockSpec((feats, blk, emb), lambda i: (0, i, 0))
    whole_up = pl.BlockSpec(cross_up.shape, lambda i: (0, 0))
    whole_down = pl.BlockSpec(cross_down.shape, lambda i: (0, 0))
    return pl.pallas_call(
        back_kernel,
        grid=(rows // blk,),
        in_specs=[part, part, part, whole_up, whole_down],
        out_specs=part,
        out_shape=jax.ShapeDtypeStruct(dx1.shape, jnp.bfloat16),
    )(dx1, x0f, cross, cross_up, cross_down)


def members(counts_row, rows):
    ends = jnp.cumsum(counts_row)
    starts = ends - counts_row
    place = jnp.arange(rows, dtype=jnp.int32)[:, None]
    return (place >= starts[None, :]) & (place < ends[None, :])


def dot_last(left, right):
    return lax.dot_general(
        left, right, (((1,), (1,)), ((), ())), preferred_element_type=jnp.float32
    )


def pair_grad(scores, member, labels):
    gain = jnp.exp2(labels.astype(jnp.float32))
    member_f = member.astype(jnp.float32)
    same = jnp.dot(member_f, member_f.T) > 0.5
    diff = gain[:, None] - gain[None, :]
    gap = scores[None, :] - scores[:, None]
    turn = jnp.where(diff > 0, jax.nn.sigmoid(gap), jax.nn.sigmoid(-gap))
    total = jnp.sum(jnp.where(same, diff * turn, 0.0), axis=1)
    seg_gain = jnp.sum(jnp.where(member, (gain - 1.0)[:, None], 0.0), axis=0)
    norm = jnp.sum(jnp.where(member, seg_gain[None, :], 0.0), axis=1)
    return -total / jnp.maximum(norm, 1.0)


DP = ("y", "c")
MP = ("z", "x")


def local(
    table,
    ids,
    counts,
    labels,
    request_home,
    user_codes,
    cross_down,
    cross_up,
    cross_bias,
    tower_weight,
    tower_bias,
):
    f32, bf16 = jnp.float32, jnp.bfloat16
    nz, nx = lax.axis_size("z"), lax.axis_size("x")
    n_mp = nz * nx
    n_dp = lax.axis_size("y") * lax.axis_size("c")
    d_idx = lax.axis_index("y") * lax.axis_size("c") + lax.axis_index("c")
    m_idx = lax.axis_index("z") * nx + lax.axis_index("x")
    rows = labels.shape[0]
    seg_count = counts.shape[1]
    width = user_codes.shape[1]
    emb = table.shape[2]
    rank = cross_down.shape[1]
    scale = 1.0 / jnp.sqrt(jnp.float32(width))

    piece = tower_weight.shape[1] // n_dp
    w_piece = lax.dynamic_slice_in_dim(tower_weight, d_idx * piece, piece, axis=1)
    w_cols = lax.all_to_all(
        jnp.broadcast_to(w_piece[None], (n_mp,) + w_piece.shape), MP, 0, 0, tiled=True
    ).reshape(n_mp * w_piece.shape[0], piece)

    held = user_codes.shape[0]
    home_local = lax.dynamic_slice_in_dim(request_home, d_idx * held, held)
    wanted = (
        (jnp.arange(n_dp, dtype=jnp.int32)[:, None] * n_mp + m_idx) * seg_count
        + jnp.arange(seg_count, dtype=jnp.int32)[None, :]
    ).reshape(-1)
    pick = (home_local[None, :] == wanted[:, None]).astype(bf16)
    mine = jnp.dot(pick, user_codes, preferred_element_type=f32).astype(bf16)

    count = ids.shape[0]
    flat_ids = jnp.transpose(ids[:, 0, :]).reshape(-1)
    pooled = pool_rows(table[0], flat_ids, count)
    w_cols, pooled = lax.optimization_barrier((w_cols, pooled))
    w_all, mine_all = lax.all_gather((w_cols, mine.reshape(-1, piece)), DP, axis=1, tiled=True)
    w3 = w_all.reshape(n_mp, emb, width)
    ride = seg_count * width // piece
    mine_all = lax.dynamic_slice_in_dim(mine_all, d_idx * ride, ride, axis=0)
    mine_all = mine_all.reshape(seg_count, width // piece, n_dp, piece)
    user_seg = jnp.sum(mine_all.astype(f32), axis=2).reshape(seg_count, width).astype(bf16)
    x0f = lax.all_to_all(pooled.reshape(n_mp, rows, emb), MP, 0, 0, tiled=True)

    member = members(counts[0], rows)
    cd3 = cross_down.reshape(n_mp, emb, rank)
    cu3 = cross_up.reshape(rank, n_mp, emb)
    bias3 = cross_bias.reshape(n_mp, 1, emb)
    z = jnp.einsum("fcd,fdr->cr", x0f, cd3, preferred_element_type=f32).astype(bf16)
    cross = jnp.einsum("cr,rfd->fcd", z, cu3, preferred_element_type=f32) + bias3
    x1 = (x0f * cross + x0f).astype(bf16)
    act = jnp.einsum("fcd,fdh->ch", x1, w3, preferred_element_type=f32) + tower_bias
    sig = jax.nn.sigmoid(act)
    hidden = (act * sig).astype(bf16)
    pair = dot_last(hidden, user_seg)
    score = jnp.sum(jnp.where(member, pair, 0.0), axis=1) * scale
    dscore = pair_grad(score, member, labels)
    code = jnp.dot(member.astype(bf16), user_seg, preferred_element_type=f32)
    slope = sig * (1.0 + act * (1.0 - sig))
    dact = (dscore[:, None] * code * scale * slope).astype(bf16)
    dx1 = jnp.einsum("ch,fdh->fcd", dact, w3, preferred_element_type=f32)
    grads = back_rows(dx1, x0f, cross, cross_up, cross_down)
    returned = lax.all_to_all(grads, MP, 0, 0, tiled=True)
    return (score, returned.reshape(n_mp * rows, 1, emb))


def split_mesh(mesh):
    grid = mesh.devices
    n_dp, n_mp = grid.shape
    try:
        nx = len({d.coords[0] for d in grid[0, :]})
        nc = len({d.core_on_chip for d in grid[:, 0]})
    except AttributeError:
        nx, nc = 1, 1
    if n_mp % nx or n_dp % nc:
        nx, nc = 1, 1
    return Mesh(grid.reshape(n_dp // nc, nc, n_mp // nx, nx), ("y", "c", "z", "x"))


def solution(mesh):
    mesh4 = split_mesh(mesh)
    in_specs = (
        P(MP, None, None),
        P(DP, MP, None),
        P(DP + MP, None),
        P(DP + MP),
        P(),
        P(DP, None),
        P(),
        P(),
        P(),
        P(MP, None),
        P(),
    )
    out_specs = (P(DP + MP), P(DP, MP, None))
    return jax.shard_map(local, mesh=mesh4, in_specs=in_specs, out_specs=out_specs, check_vma=False)
```

```python
import jax
import jax.numpy as jnp
from jax import lax
from jax.experimental import pallas as pl
from jax.experimental.pallas import tpu as pltpu
from jax.sharding import Mesh, PartitionSpec as P


def pool_kernel(ids_ref, tab_ref, out_ref, tabf, acc):
    step = pl.program_id(0)
    blk = out_ref.shape[0]
    total = ids_ref.shape[0] // 2

    @pl.when(step == 0)
    def _():
        tabf[...] = tab_ref[...].astype(jnp.float32)

    base = step * blk

    def body(j, carry):
        for u in range(8):
            c = j * 8 + u
            a = ids_ref[base + c]
            b = ids_ref[total + base + c]
            acc[pl.ds(c, 1), :] = tabf[pl.ds(a, 1), :] + tabf[pl.ds(b, 1), :]
        return carry

    lax.fori_loop(0, blk // 8, body, 0)
    out_ref[...] = acc[...].astype(out_ref.dtype)


def pool_rows(slab, flat_ids, count, blk=1024):
    slab_rows, emb = slab.shape
    spec = pltpu.PrefetchScalarGridSpec(
        num_scalar_prefetch=1,
        grid=(count // blk,),
        in_specs=[pl.BlockSpec((slab_rows, emb), lambda i, ids: (0, 0))],
        out_specs=pl.BlockSpec((blk, emb), lambda i, ids: (i, 0)),
        scratch_shapes=[
            pltpu.VMEM((slab_rows, emb), jnp.float32),
            pltpu.VMEM((blk, emb), jnp.float32),
        ],
    )
    return pl.pallas_call(
        pool_kernel,
        grid_spec=spec,
        out_shape=jax.ShapeDtypeStruct((count, emb), slab.dtype),
    )(flat_ids, slab)


def back_kernel(dx1_ref, x0_ref, cross_ref, up_ref, down_ref, out_ref):
    feats, _, emb = dx1_ref.shape

    def down_pass(f, acc):
        rows = pl.ds(pl.multiple_of(f * emb, emb), emb)
        dcross = (dx1_ref[f] * x0_ref[f].astype(jnp.float32)).astype(jnp.bfloat16)
        return acc + jnp.dot(dcross, up_ref[rows, :], preferred_element_type=jnp.float32)

    acc = jnp.zeros((dx1_ref.shape[1], up_ref.shape[1]), jnp.float32)
    dz = lax.fori_loop(0, feats, down_pass, acc).astype(jnp.bfloat16)

    def up_pass(f, carry):
        cols = pl.ds(pl.multiple_of(f * emb, emb), emb)
        back = jnp.dot(dz, down_ref[:, cols], preferred_element_type=jnp.float32)
        out_ref[f] = (dx1_ref[f] * (1.0 + cross_ref[f]) + back).astype(out_ref.dtype)
        return carry

    lax.fori_loop(0, feats, up_pass, 0)


def back_rows(dx1, x0f, cross, cross_up, cross_down, blk=128):
    feats, rows, emb = dx1.shape
    part = pl.BlockSpec((feats, blk, emb), lambda i: (0, i, 0))
    whole_up = pl.BlockSpec(cross_up.shape, lambda i: (0, 0))
    whole_down = pl.BlockSpec(cross_down.shape, lambda i: (0, 0))
    return pl.pallas_call(
        back_kernel,
        grid=(rows // blk,),
        in_specs=[part, part, part, whole_up, whole_down],
        out_specs=part,
        out_shape=jax.ShapeDtypeStruct(dx1.shape, jnp.bfloat16),
    )(dx1, x0f, cross, cross_up, cross_down)


def members(counts_row, rows):
    ends = jnp.cumsum(counts_row)
    starts = ends - counts_row
    place = jnp.arange(rows, dtype=jnp.int32)[:, None]
    return (place >= starts[None, :]) & (place < ends[None, :])


def dot_last(left, right):
    return lax.dot_general(
        left, right, (((1,), (1,)), ((), ())), preferred_element_type=jnp.float32
    )


def pair_grad(scores, member, labels):
    gain = jnp.exp2(labels.astype(jnp.float32))
    member_f = member.astype(jnp.float32)
    same = jnp.dot(member_f, member_f.T) > 0.5
    diff = gain[:, None] - gain[None, :]
    gap = scores[None, :] - scores[:, None]
    turn = jnp.where(diff > 0, jax.nn.sigmoid(gap), jax.nn.sigmoid(-gap))
    total = jnp.sum(jnp.where(same, diff * turn, 0.0), axis=1)
    seg_gain = jnp.sum(jnp.where(member, (gain - 1.0)[:, None], 0.0), axis=0)
    norm = jnp.sum(jnp.where(member, seg_gain[None, :], 0.0), axis=1)
    return -total / jnp.maximum(norm, 1.0)


DP = ("y", "c")
MP = ("z", "x")


def local(
    table,
    ids,
    counts,
    labels,
    request_home,
    user_codes,
    cross_down,
    cross_up,
    cross_bias,
    tower_weight,
    tower_bias,
):
    f32, bf16 = jnp.float32, jnp.bfloat16
    nz, nx = lax.axis_size("z"), lax.axis_size("x")
    n_mp = nz * nx
    n_dp = lax.axis_size("y") * lax.axis_size("c")
    d_idx = lax.axis_index("y") * lax.axis_size("c") + lax.axis_index("c")
    m_idx = lax.axis_index("z") * nx + lax.axis_index("x")
    rows = labels.shape[0]
    seg_count = counts.shape[1]
    width = user_codes.shape[1]
    emb = table.shape[2]
    rank = cross_down.shape[1]
    scale = 1.0 / jnp.sqrt(jnp.float32(width))

    piece = tower_weight.shape[1] // n_dp
    w_piece = lax.dynamic_slice_in_dim(tower_weight, d_idx * piece, piece, axis=1)
    w_cols = lax.all_to_all(
        jnp.broadcast_to(w_piece[None], (n_mp,) + w_piece.shape), MP, 0, 0, tiled=True
    ).reshape(n_mp * w_piece.shape[0], piece)

    held = user_codes.shape[0]
    home_local = lax.dynamic_slice_in_dim(request_home, d_idx * held, held)
    wanted = (
        (jnp.arange(n_dp, dtype=jnp.int32)[:, None] * n_mp + m_idx) * seg_count
        + jnp.arange(seg_count, dtype=jnp.int32)[None, :]
    ).reshape(-1)
    pick = (home_local[None, :] == wanted[:, None]).astype(bf16)
    mine = jnp.dot(pick, user_codes, preferred_element_type=f32).astype(bf16)

    count = ids.shape[0]
    flat_ids = jnp.transpose(ids[:, 0, :]).reshape(-1)
    pooled = pool_rows(table[0], flat_ids, count)
    w_cols, pooled = lax.optimization_barrier((w_cols, pooled))
    w_all, mine_all = lax.all_gather((w_cols, mine.reshape(-1, piece)), DP, axis=1, tiled=True)
    w3 = w_all.reshape(n_mp, emb, width)
    ride = seg_count * width // piece
    mine_all = lax.dynamic_slice_in_dim(mine_all, d_idx * ride, ride, axis=0)
    mine_all = mine_all.reshape(seg_count, width // piece, n_dp, piece)
    user_seg = jnp.sum(mine_all.astype(f32), axis=2).reshape(seg_count, width).astype(bf16)
    x0f = lax.all_to_all(pooled.reshape(n_mp, rows, emb), MP, 0, 0, tiled=True)

    member = members(counts[0], rows)
    cd3 = cross_down.reshape(n_mp, emb, rank)
    cu3 = cross_up.reshape(rank, n_mp, emb)
    bias3 = cross_bias.reshape(n_mp, 1, emb)
    z = jnp.einsum("fcd,fdr->cr", x0f, cd3, preferred_element_type=f32).astype(bf16)
    cross = jnp.einsum("cr,rfd->fcd", z, cu3, preferred_element_type=f32) + bias3
    x1 = (x0f * cross + x0f).astype(bf16)
    act = jnp.einsum("fcd,fdh->ch", x1, w3, preferred_element_type=f32) + tower_bias
    sig = jax.nn.sigmoid(act)
    hidden = (act * sig).astype(bf16)
    pair = dot_last(hidden, user_seg)
    score = jnp.sum(jnp.where(member, pair, 0.0), axis=1) * scale
    dscore = pair_grad(score, member, labels)
    code = jnp.dot(member.astype(bf16), user_seg, preferred_element_type=f32)
    slope = sig * (1.0 + act * (1.0 - sig))
    dact = (dscore[:, None] * code * scale * slope).astype(bf16)
    dx1 = jnp.einsum("ch,fdh->fcd", dact, w3, preferred_element_type=f32)
    grads = back_rows(dx1, x0f, cross, cross_up.T, cross_down.T)
    returned = lax.all_to_all(grads, MP, 0, 0, tiled=True)
    return (score, returned.reshape(n_mp * rows, 1, emb))


def split_mesh(mesh):
    grid = mesh.devices
    n_dp, n_mp = grid.shape
    try:
        nx = len({d.coords[0] for d in grid[0, :]})
        nc = len({d.core_on_chip for d in grid[:, 0]})
    except AttributeError:
        nx, nc = 1, 1
    if n_mp % nx or n_dp % nc:
        nx, nc = 1, 1
    return Mesh(grid.reshape(n_dp // nc, nc, n_mp // nx, nx), ("y", "c", "z", "x"))


def solution(mesh):
    mesh4 = split_mesh(mesh)
    in_specs = (
        P(MP, None, None),
        P(DP, MP, None),
        P(DP + MP, None),
        P(DP + MP),
        P(),
        P(DP, None),
        P(),
        P(),
        P(),
        P(MP, None),
        P(),
    )
    out_specs = (P(DP + MP), P(DP, MP, None))
    return jax.shard_map(local, mesh=mesh4, in_specs=in_specs, out_specs=out_specs, check_vma=False)
```

```python
import jax
import jax.numpy as jnp
from jax import lax
from jax.experimental import pallas as pl
from jax.experimental.pallas import tpu as pltpu
from jax.sharding import Mesh, PartitionSpec as P


def pool_kernel(ids_ref, tab_ref, out_ref, tabf, acc):
    step = pl.program_id(0)
    blk = out_ref.shape[0]
    total = ids_ref.shape[0] // 2

    @pl.when(step == 0)
    def _():
        tabf[...] = tab_ref[...].astype(jnp.float32)

    base = step * blk

    def body(j, carry):
        for u in range(8):
            c = j * 8 + u
            a = ids_ref[base + c]
            b = ids_ref[total + base + c]
            acc[pl.ds(c, 1), :] = tabf[pl.ds(a, 1), :] + tabf[pl.ds(b, 1), :]
        return carry

    lax.fori_loop(0, blk // 8, body, 0)
    out_ref[...] = acc[...].astype(out_ref.dtype)


def pool_rows(slab, flat_ids, count, blk=1024):
    slab_rows, emb = slab.shape
    spec = pltpu.PrefetchScalarGridSpec(
        num_scalar_prefetch=1,
        grid=(count // blk,),
        in_specs=[pl.BlockSpec((slab_rows, emb), lambda i, ids: (0, 0))],
        out_specs=pl.BlockSpec((blk, emb), lambda i, ids: (i, 0)),
        scratch_shapes=[
            pltpu.VMEM((slab_rows, emb), jnp.float32),
            pltpu.VMEM((blk, emb), jnp.float32),
        ],
    )
    return pl.pallas_call(
        pool_kernel,
        grid_spec=spec,
        out_shape=jax.ShapeDtypeStruct((count, emb), slab.dtype),
    )(flat_ids, slab)


def members(counts_row, rows):
    ends = jnp.cumsum(counts_row)
    starts = ends - counts_row
    place = jnp.arange(rows, dtype=jnp.int32)[:, None]
    return (place >= starts[None, :]) & (place < ends[None, :])


def dot_last(left, right):
    return lax.dot_general(
        left, right, (((1,), (1,)), ((), ())), preferred_element_type=jnp.float32
    )


def pair_grad(scores, member, labels):
    gain = jnp.exp2(labels.astype(jnp.float32))
    member_f = member.astype(jnp.float32)
    same = jnp.dot(member_f, member_f.T) > 0.5
    diff = gain[:, None] - gain[None, :]
    gap = scores[None, :] - scores[:, None]
    turn = jnp.where(diff > 0, jax.nn.sigmoid(gap), jax.nn.sigmoid(-gap))
    total = jnp.sum(jnp.where(same, diff * turn, 0.0), axis=1)
    seg_gain = jnp.sum(jnp.where(member, (gain - 1.0)[:, None], 0.0), axis=0)
    norm = jnp.sum(jnp.where(member, seg_gain[None, :], 0.0), axis=1)
    return -total / jnp.maximum(norm, 1.0)


DP = ("y", "c")
MP = ("z", "x")


def local(
    table,
    ids,
    counts,
    labels,
    request_home,
    user_codes,
    cross_down,
    cross_up,
    cross_bias,
    tower_weight,
    tower_bias,
):
    f32, bf16 = jnp.float32, jnp.bfloat16
    nz, nx = lax.axis_size("z"), lax.axis_size("x")
    n_mp = nz * nx
    n_dp = lax.axis_size("y") * lax.axis_size("c")
    d_idx = lax.axis_index("y") * lax.axis_size("c") + lax.axis_index("c")
    m_idx = lax.axis_index("z") * nx + lax.axis_index("x")
    rows = labels.shape[0]
    seg_count = counts.shape[1]
    width = user_codes.shape[1]
    emb = table.shape[2]
    rank = cross_down.shape[1]
    scale = 1.0 / jnp.sqrt(jnp.float32(width))

    piece = tower_weight.shape[1] // n_dp
    w_piece = lax.dynamic_slice_in_dim(tower_weight, d_idx * piece, piece, axis=1)
    w_cols = lax.all_to_all(
        jnp.broadcast_to(w_piece[None], (n_mp,) + w_piece.shape), MP, 0, 0, tiled=True
    ).reshape(n_mp * w_piece.shape[0], piece)

    held = user_codes.shape[0]
    home_local = lax.dynamic_slice_in_dim(request_home, d_idx * held, held)
    wanted = (
        (jnp.arange(n_dp, dtype=jnp.int32)[:, None] * n_mp + m_idx) * seg_count
        + jnp.arange(seg_count, dtype=jnp.int32)[None, :]
    ).reshape(-1)
    pick = (home_local[None, :] == wanted[:, None]).astype(bf16)
    mine = jnp.dot(pick, user_codes, preferred_element_type=f32).astype(bf16)

    count = ids.shape[0]
    flat_ids = jnp.transpose(ids[:, 0, :]).reshape(-1)
    pooled = pool_rows(table[0], flat_ids, count)
    w_cols, pooled = lax.optimization_barrier((w_cols, pooled))
    w_all, mine_all = lax.all_gather((w_cols, mine.reshape(-1, piece)), DP, axis=1, tiled=True)
    w3 = w_all.reshape(n_mp, emb, width)
    ride = seg_count * width // piece
    mine_all = lax.dynamic_slice_in_dim(mine_all, d_idx * ride, ride, axis=0)
    mine_all = mine_all.reshape(seg_count, width // piece, n_dp, piece)
    user_seg = jnp.sum(mine_all.astype(f32), axis=2).reshape(seg_count, width).astype(bf16)
    x0f = lax.all_to_all(pooled.reshape(n_mp, rows, emb), MP, 0, 0, tiled=True)

    member = members(counts[0], rows)
    cd3 = cross_down.reshape(n_mp, emb, rank)
    cu3 = cross_up.reshape(rank, n_mp, emb)
    bias3 = cross_bias.reshape(n_mp, 1, emb)
    z = jnp.einsum("fcd,fdr->cr", x0f, cd3, preferred_element_type=f32).astype(bf16)
    cross = (jnp.einsum("cr,rfd->fcd", z, cu3, preferred_element_type=f32) + bias3).astype(bf16)
    x0w = x0f.astype(f32)
    x1 = (x0w * cross.astype(f32) + x0w).astype(bf16)
    act = jnp.einsum("fcd,fdh->ch", x1, w3, preferred_element_type=f32) + tower_bias
    sig = jax.nn.sigmoid(act)
    hidden = (act * sig).astype(bf16)
    pair = dot_last(hidden, user_seg)
    score = jnp.sum(jnp.where(member, pair, 0.0), axis=1) * scale
    dscore = pair_grad(score, member, labels)
    code = jnp.dot(member.astype(bf16), user_seg, preferred_element_type=f32)
    slope = sig * (1.0 + act * (1.0 - sig))
    dact = (dscore[:, None] * code * scale * slope).astype(bf16)
    dx1 = jnp.einsum("ch,fdh->fcd", dact, w3, preferred_element_type=f32).astype(bf16)
    dx1 = dx1.astype(f32)
    dcross = (dx1 * x0w).astype(bf16)
    dz = jnp.einsum("fcd,rfd->cr", dcross, cu3, preferred_element_type=f32).astype(bf16)
    dx0 = dx1 * (1.0 + cross.astype(f32)) + jnp.einsum(
        "cr,fdr->fcd", dz, cd3, preferred_element_type=f32
    )
    grads = dx0.astype(bf16)
    returned = lax.all_to_all(grads, MP, 0, 0, tiled=True)
    return (score, returned.reshape(n_mp * rows, 1, emb))


def split_mesh(mesh):
    grid = mesh.devices
    n_dp, n_mp = grid.shape
    try:
        nx = len({d.coords[0] for d in grid[0, :]})
        nc = len({d.core_on_chip for d in grid[:, 0]})
    except AttributeError:
        nx, nc = 1, 1
    if n_mp % nx or n_dp % nc:
        nx, nc = 1, 1
    return Mesh(grid.reshape(n_dp // nc, nc, n_mp // nx, nx), ("y", "c", "z", "x"))


def solution(mesh):
    mesh4 = split_mesh(mesh)
    in_specs = (
        P(MP, None, None),
        P(DP, MP, None),
        P(DP + MP, None),
        P(DP + MP),
        P(),
        P(DP, None),
        P(),
        P(),
        P(),
        P(MP, None),
        P(),
    )
    out_specs = (P(DP + MP), P(DP, MP, None))
    return jax.shard_map(local, mesh=mesh4, in_specs=in_specs, out_specs=out_specs, check_vma=False)
```

```python
import jax
import jax.numpy as jnp
from jax import lax
from jax.experimental import pallas as pl
from jax.experimental.pallas import tpu as pltpu
from jax.sharding import Mesh, PartitionSpec as P


def pool_kernel(ids_ref, tab_ref, out_ref, tabf, acc):
    step = pl.program_id(0)
    blk = out_ref.shape[0]
    total = ids_ref.shape[0] // 2

    @pl.when(step == 0)
    def _():
        tabf[...] = tab_ref[...].astype(jnp.float32)

    base = step * blk

    def body(j, carry):
        for u in range(8):
            c = j * 8 + u
            a = ids_ref[base + c]
            b = ids_ref[total + base + c]
            acc[pl.ds(c, 1), :] = tabf[pl.ds(a, 1), :] + tabf[pl.ds(b, 1), :]
        return carry

    lax.fori_loop(0, blk // 8, body, 0)
    out_ref[...] = acc[...].astype(out_ref.dtype)


def pool_rows(slab, flat_ids, count, blk=1024):
    slab_rows, emb = slab.shape
    spec = pltpu.PrefetchScalarGridSpec(
        num_scalar_prefetch=1,
        grid=(count // blk,),
        in_specs=[pl.BlockSpec((slab_rows, emb), lambda i, ids: (0, 0))],
        out_specs=pl.BlockSpec((blk, emb), lambda i, ids: (i, 0)),
        scratch_shapes=[
            pltpu.VMEM((slab_rows, emb), jnp.float32),
            pltpu.VMEM((blk, emb), jnp.float32),
        ],
    )
    return pl.pallas_call(
        pool_kernel,
        grid_spec=spec,
        out_shape=jax.ShapeDtypeStruct((count, emb), slab.dtype),
    )(flat_ids, slab)


def members(counts_row, rows):
    ends = jnp.cumsum(counts_row)
    starts = ends - counts_row
    place = jnp.arange(rows, dtype=jnp.int32)[:, None]
    return (place >= starts[None, :]) & (place < ends[None, :])


def dot_last(left, right):
    return lax.dot_general(
        left, right, (((1,), (1,)), ((), ())), preferred_element_type=jnp.float32
    )


def pair_grad(scores, member, labels):
    gain = jnp.exp2(labels.astype(jnp.float32))
    member_f = member.astype(jnp.float32)
    same = jnp.dot(member_f, member_f.T) > 0.5
    diff = gain[:, None] - gain[None, :]
    gap = scores[None, :] - scores[:, None]
    turn = jnp.where(diff > 0, jax.nn.sigmoid(gap), jax.nn.sigmoid(-gap))
    total = jnp.sum(jnp.where(same, diff * turn, 0.0), axis=1)
    seg_gain = jnp.sum(jnp.where(member, (gain - 1.0)[:, None], 0.0), axis=0)
    norm = jnp.sum(jnp.where(member, seg_gain[None, :], 0.0), axis=1)
    return -total / jnp.maximum(norm, 1.0)


DP = ("y", "c")
MP = ("z", "x")


def local(
    table,
    ids,
    counts,
    labels,
    request_home,
    user_codes,
    cross_down,
    cross_up,
    cross_bias,
    tower_weight,
    tower_bias,
):
    f32, bf16 = jnp.float32, jnp.bfloat16
    nz, nx = lax.axis_size("z"), lax.axis_size("x")
    n_mp = nz * nx
    n_dp = lax.axis_size("y") * lax.axis_size("c")
    d_idx = lax.axis_index("y") * lax.axis_size("c") + lax.axis_index("c")
    m_idx = lax.axis_index("z") * nx + lax.axis_index("x")
    rows = labels.shape[0]
    seg_count = counts.shape[1]
    width = user_codes.shape[1]
    emb = table.shape[2]
    rank = cross_down.shape[1]
    scale = 1.0 / jnp.sqrt(jnp.float32(width))

    piece = tower_weight.shape[1] // n_dp
    w_piece = lax.dynamic_slice_in_dim(tower_weight, d_idx * piece, piece, axis=1)
    w_cols = lax.all_to_all(
        jnp.broadcast_to(w_piece[None], (n_mp,) + w_piece.shape), MP, 0, 0, tiled=True
    ).reshape(n_mp * w_piece.shape[0], piece)

    held = user_codes.shape[0]
    home_local = lax.dynamic_slice_in_dim(request_home, d_idx * held, held)
    wanted = (
        (jnp.arange(n_dp, dtype=jnp.int32)[:, None] * n_mp + m_idx) * seg_count
        + jnp.arange(seg_count, dtype=jnp.int32)[None, :]
    ).reshape(-1)
    pick = (home_local[None, :] == wanted[:, None]).astype(bf16)
    mine = jnp.dot(pick, user_codes, preferred_element_type=f32).astype(bf16)

    count = ids.shape[0]
    flat_ids = jnp.transpose(ids[:, 0, :]).reshape(-1)
    pooled = pool_rows(table[0], flat_ids, count)
    w_cols, pooled = lax.optimization_barrier((w_cols, pooled))
    w_all, mine_all = lax.all_gather((w_cols, mine.reshape(-1, piece)), DP, axis=1, tiled=True)
    w3 = w_all.reshape(n_mp, emb, width)
    ride = seg_count * width // piece
    mine_all = lax.dynamic_slice_in_dim(mine_all, d_idx * ride, ride, axis=0)
    mine_all = mine_all.reshape(seg_count, width // piece, n_dp, piece)
    user_seg = jnp.sum(mine_all.astype(f32), axis=2).reshape(seg_count, width).astype(bf16)
    x0f = lax.all_to_all(pooled.reshape(n_mp, rows, emb), MP, 0, 0, tiled=True)

    member = members(counts[0], rows)
    cd3 = cross_down.reshape(n_mp, emb, rank)
    cu3 = cross_up.reshape(rank, n_mp, emb)
    bias3 = cross_bias.reshape(n_mp, 1, emb)
    z = jnp.einsum("fcd,fdr->cr", x0f, cd3, preferred_element_type=f32).astype(bf16)
    cross = jnp.einsum("cr,rfd->fcd", z, cu3, preferred_element_type=f32) + bias3
    x1 = (x0f * cross + x0f).astype(bf16)
    act = jnp.einsum("fcd,fdh->ch", x1, w3, preferred_element_type=f32) + tower_bias
    sig = jax.nn.sigmoid(act)
    hidden = (act * sig).astype(bf16)
    pair = dot_last(hidden, user_seg)
    score = jnp.sum(jnp.where(member, pair, 0.0), axis=1) * scale
    dscore = pair_grad(score, member, labels)
    code = jnp.dot(member.astype(bf16), user_seg, preferred_element_type=f32)
    slope = sig * (1.0 + act * (1.0 - sig))
    dact = (dscore[:, None] * code * scale * slope).astype(bf16)
    dx1 = jnp.einsum("ch,fdh->fcd", dact, w3, preferred_element_type=f32).astype(bf16)
    dx1 = dx1.astype(f32)
    dcross = (dx1 * x0f).astype(bf16)
    dz = jnp.einsum("fcd,rfd->cr", dcross, cu3, preferred_element_type=f32).astype(bf16)
    dx0 = dx1 * (1.0 + cross) + jnp.einsum(
        "cr,fdr->fcd", dz, cd3, preferred_element_type=f32
    )
    grads = dx0.astype(bf16)
    returned = lax.all_to_all(grads, MP, 0, 0, tiled=True)
    return (score, returned.reshape(n_mp * rows, 1, emb))


def split_mesh(mesh):
    grid = mesh.devices
    n_dp, n_mp = grid.shape
    try:
        nx = len({d.coords[0] for d in grid[0, :]})
        nc = len({d.core_on_chip for d in grid[:, 0]})
    except AttributeError:
        nx, nc = 1, 1
    if n_mp % nx or n_dp % nc:
        nx, nc = 1, 1
    return Mesh(grid.reshape(n_dp // nc, nc, n_mp // nx, nx), ("y", "c", "z", "x"))


def solution(mesh):
    mesh4 = split_mesh(mesh)
    in_specs = (
        P(MP, None, None),
        P(DP, MP, None),
        P(DP + MP, None),
        P(DP + MP),
        P(),
        P(DP, None),
        P(),
        P(),
        P(),
        P(MP, None),
        P(),
    )
    out_specs = (P(DP + MP), P(DP, MP, None))
    return jax.shard_map(local, mesh=mesh4, in_specs=in_specs, out_specs=out_specs, check_vma=False)
```

```python
import jax
import jax.numpy as jnp
from jax import lax
from jax.experimental import pallas as pl
from jax.experimental.pallas import tpu as pltpu
from jax.sharding import Mesh, PartitionSpec as P


def pool_kernel(ids_ref, tab_ref, out_ref, tabf, acc):
    step = pl.program_id(0)
    blk = out_ref.shape[0]
    total = ids_ref.shape[0] // 2

    @pl.when(step == 0)
    def _():
        tabf[...] = tab_ref[...].astype(jnp.float32)

    base = step * blk

    def body(j, carry):
        for u in range(8):
            c = j * 8 + u
            a = ids_ref[base + c]
            b = ids_ref[total + base + c]
            acc[pl.ds(c, 1), :] = tabf[pl.ds(a, 1), :] + tabf[pl.ds(b, 1), :]
        return carry

    lax.fori_loop(0, blk // 8, body, 0)
    out_ref[...] = acc[...].astype(out_ref.dtype)


def pool_rows(slab, flat_ids, count, blk=1024):
    slab_rows, emb = slab.shape
    spec = pltpu.PrefetchScalarGridSpec(
        num_scalar_prefetch=1,
        grid=(count // blk,),
        in_specs=[pl.BlockSpec((slab_rows, emb), lambda i, ids: (0, 0))],
        out_specs=pl.BlockSpec((blk, emb), lambda i, ids: (i, 0)),
        scratch_shapes=[
            pltpu.VMEM((slab_rows, emb), jnp.float32),
            pltpu.VMEM((blk, emb), jnp.float32),
        ],
    )
    return pl.pallas_call(
        pool_kernel,
        grid_spec=spec,
        out_shape=jax.ShapeDtypeStruct((count, emb), slab.dtype),
    )(flat_ids, slab)


def members(counts_row, rows):
    ends = jnp.cumsum(counts_row)
    starts = ends - counts_row
    place = jnp.arange(rows, dtype=jnp.int32)[:, None]
    return (place >= starts[None, :]) & (place < ends[None, :])


def dot_last(left, right):
    return lax.dot_general(
        left, right, (((1,), (1,)), ((), ())), preferred_element_type=jnp.float32
    )


def pair_grad(scores, member, labels):
    gain = jnp.exp2(labels.astype(jnp.float32))
    member_f = member.astype(jnp.float32)
    same = jnp.dot(member_f, member_f.T) > 0.5
    diff = gain[:, None] - gain[None, :]
    gap = scores[None, :] - scores[:, None]
    turn = jnp.where(diff > 0, jax.nn.sigmoid(gap), jax.nn.sigmoid(-gap))
    total = jnp.sum(jnp.where(same, diff * turn, 0.0), axis=1)
    seg_gain = jnp.sum(jnp.where(member, (gain - 1.0)[:, None], 0.0), axis=0)
    norm = jnp.sum(jnp.where(member, seg_gain[None, :], 0.0), axis=1)
    return -total / jnp.maximum(norm, 1.0)


DP = ("y", "c")
MP = ("z", "x")


def local(
    table,
    ids,
    counts,
    labels,
    request_home,
    user_codes,
    cross_down,
    cross_up,
    cross_bias,
    tower_weight,
    tower_bias,
):
    f32, bf16 = jnp.float32, jnp.bfloat16
    nz, nx = lax.axis_size("z"), lax.axis_size("x")
    n_mp = nz * nx
    n_dp = lax.axis_size("y") * lax.axis_size("c")
    d_idx = lax.axis_index("y") * lax.axis_size("c") + lax.axis_index("c")
    m_idx = lax.axis_index("z") * nx + lax.axis_index("x")
    rows = labels.shape[0]
    seg_count = counts.shape[1]
    width = user_codes.shape[1]
    emb = table.shape[2]
    rank = cross_down.shape[1]
    scale = 1.0 / jnp.sqrt(jnp.float32(width))

    piece = tower_weight.shape[1] // n_dp
    w_piece = lax.dynamic_slice_in_dim(tower_weight, d_idx * piece, piece, axis=1)
    w_cols = lax.all_to_all(
        jnp.broadcast_to(w_piece[None], (n_mp,) + w_piece.shape), MP, 0, 0, tiled=True
    ).reshape(n_mp * w_piece.shape[0], piece)

    held = user_codes.shape[0]
    home_local = lax.dynamic_slice_in_dim(request_home, d_idx * held, held)
    wanted = (
        (jnp.arange(n_dp, dtype=jnp.int32)[:, None] * n_mp + m_idx) * seg_count
        + jnp.arange(seg_count, dtype=jnp.int32)[None, :]
    ).reshape(-1)
    pick = (home_local[None, :] == wanted[:, None]).astype(bf16)
    mine = jnp.dot(pick, user_codes, preferred_element_type=f32).astype(bf16)

    count = ids.shape[0]
    flat_ids = jnp.transpose(ids[:, 0, :]).reshape(-1)
    pooled = pool_rows(table[0], flat_ids, count)
    w_cols, pooled = lax.optimization_barrier((w_cols, pooled))
    w_all, mine_all = lax.all_gather((w_cols, mine.reshape(-1, piece)), DP, axis=1, tiled=True)
    w3 = w_all.reshape(n_mp, emb, width)
    ride = seg_count * width // piece
    mine_all = lax.dynamic_slice_in_dim(mine_all, d_idx * ride, ride, axis=0)
    mine_all = mine_all.reshape(seg_count, width // piece, n_dp, piece)
    user_seg = jnp.sum(mine_all.astype(f32), axis=2).reshape(seg_count, width).astype(bf16)
    x0f = lax.all_to_all(pooled.reshape(n_mp, rows, emb), MP, 0, 0, tiled=True)

    member = members(counts[0], rows)
    cd3 = cross_down.reshape(n_mp, emb, rank)
    cu3 = cross_up.reshape(rank, n_mp, emb)
    bias3 = cross_bias.reshape(n_mp, 1, emb)
    z = jnp.einsum("fcd,fdr->cr", x0f, cd3, preferred_element_type=f32).astype(bf16)
    cross = jnp.einsum("cr,rfd->fcd", z, cu3, preferred_element_type=f32) + bias3
    x1 = lax.optimization_barrier((x0f * cross + x0f).astype(bf16))
    act = jnp.einsum("fcd,fdh->ch", x1, w3, preferred_element_type=f32) + tower_bias
    sig = jax.nn.sigmoid(act)
    hidden = (act * sig).astype(bf16)
    pair = dot_last(hidden, user_seg)
    score = jnp.sum(jnp.where(member, pair, 0.0), axis=1) * scale
    dscore = pair_grad(score, member, labels)
    code = jnp.dot(member.astype(bf16), user_seg, preferred_element_type=f32)
    slope = sig * (1.0 + act * (1.0 - sig))
    dact = (dscore[:, None] * code * scale * slope).astype(bf16)
    dx1 = jnp.einsum("ch,fdh->fcd", dact, w3, preferred_element_type=f32).astype(bf16)
    dx1 = dx1.astype(f32)
    dcross = (dx1 * x0f).astype(bf16)
    dz = jnp.einsum("fcd,rfd->cr", dcross, cu3, preferred_element_type=f32).astype(bf16)
    dx0 = dx1 * (1.0 + cross) + jnp.einsum(
        "cr,fdr->fcd", dz, cd3, preferred_element_type=f32
    )
    grads = dx0.astype(bf16)
    returned = lax.all_to_all(grads, MP, 0, 0, tiled=True)
    return (score, returned.reshape(n_mp * rows, 1, emb))


def split_mesh(mesh):
    grid = mesh.devices
    n_dp, n_mp = grid.shape
    try:
        nx = len({d.coords[0] for d in grid[0, :]})
        nc = len({d.core_on_chip for d in grid[:, 0]})
    except AttributeError:
        nx, nc = 1, 1
    if n_mp % nx or n_dp % nc:
        nx, nc = 1, 1
    return Mesh(grid.reshape(n_dp // nc, nc, n_mp // nx, nx), ("y", "c", "z", "x"))


def solution(mesh):
    mesh4 = split_mesh(mesh)
    in_specs = (
        P(MP, None, None),
        P(DP, MP, None),
        P(DP + MP, None),
        P(DP + MP),
        P(),
        P(DP, None),
        P(),
        P(),
        P(),
        P(MP, None),
        P(),
    )
    out_specs = (P(DP + MP), P(DP, MP, None))
    return jax.shard_map(local, mesh=mesh4, in_specs=in_specs, out_specs=out_specs, check_vma=False)
```
